512 devices in a mesh: trk: 128 (over x, z, core), cam: 4 (over y).
Axes of the slice: x: 4, y: 4, z: 16, core: 2. Of those that a mesh axis runs over, the one named last changes fastest.
Arguments:
- residuals: float32 [2, 393216], P(None, ('trk', 'cam')), may hold values from -6 to 6
- camera_jac: float32 [18, 393216], P(None, ('trk', 'cam')), may hold values from -9 to 9
- point_jac: float32 [6, 393216], P(None, ('trk', 'cam')), may hold values from -6 to 6
- obs_index: int32 [3, 393216], P(None, ('trk', 'cam')), may hold values from 0 to 4095, as said below
- damping: float32 [32768], P('trk'), may hold values from 0.5 to 4
Outputs:
- elimination_tiles: float32 [128, 4, 7, 20736], P('trk', 'cam')
The draws below stay inside these ranges and needn't reach their ends.
Inputs may be any that keep to these rules, and one draw needn't show every extreme that they name: For each c and e, the values obs_index[0, n] of the rows n = ((t * 4 + c) * 128 + e) * 6 + q over all t and q are a permutation of 0 to 767. The camera obs_index[1, n] of such a row lies in a block (camera // 16) among 2 * e to 2 * e + 7, taken modulo 256. obs_index[2, n] is 1 for a live observation and 0 for a padded slot.
All inputs are finite; a program needn't handle non-finite values.
Results may differ from the reference program's by a relative error of at most 0.0003.
Values sent between devices are 32-bit elements; how exact they have to be, the bound alone decides.
No kernel may reach another device: no remote copies, remote signals or barrier semaphores. Data moves between devices by JAX's collectives and lax.ppermute only.
A program may use at most 64 MiB of HBM per device.

```python
import math
import jax
import jax.numpy as jnp
from jax import lax

CAMERAS_PER_BLK = 16
TS = 144
HOPS = 3
WIN = 8
TILE_OWN = 7
SLOTS = 12
KC = 3
TRK_DEV = 256
SPR = 6
TRACKS = 32768
ROWS = 393216
CAMERA_BLOCKS = 256
N_TRK = 128
N_CAM = 4


def draw_obs_index(key, part):
    key_shuffle = jax.random.fold_in(key, 11)
    key_block = jax.random.fold_in(key, 12)
    camera_key_value = jax.random.fold_in(key, 13)
    key_alive = jax.random.fold_in(key, 14)
    row_keys = jax.random.split(key_shuffle, N_CAM * N_TRK)

    def shuffle(single_key):
        return jax.random.permutation(single_key, TRK_DEV * KC)
    shuffled = jax.vmap(shuffle)(row_keys).reshape((N_CAM, N_TRK, N_TRK, SPR))
    position = jnp.transpose(shuffled, (2, 0, 1, 3)).astype(jnp.int32)
    launch_layout = (N_TRK, N_CAM, N_TRK, SPR)
    offset = jax.random.randint(key_block, launch_layout, 0, WIN)
    offset = offset.at[0, 0, N_TRK - 1, 0].set(1)
    target = 2 * jnp.arange(N_TRK, dtype=jnp.int32)[None, None, :, None]
    block_number = jnp.mod(target + offset, CAMERA_BLOCKS)
    within = jax.random.randint(camera_key_value, launch_layout, 0, CAMERAS_PER_BLK)
    within = within.at[0, 0, N_TRK - 1, 0].set(CAMERAS_PER_BLK - 1)
    camera_view = block_number * CAMERAS_PER_BLK + within
    alive_mask = (jax.random.randint(key_alive, launch_layout, 0, 4) > 0).astype(jnp.int32)
    return jnp.stack([position, camera_view.astype(jnp.int32), alive_mask]).reshape((3, -1)).astype(jnp.int32)


def shard_levels(own_key, shape, pieces, low, top_value):
    def one(dim, blocks):
        draws = jax.random.uniform(jax.random.fold_in(jax.random.fold_in(own_key, 6), dim), (blocks,), jnp.float32, low / len(pieces), top_value / len(pieces))
        return jnp.repeat(jnp.exp(draws), shape[dim] // blocks).reshape((-1,) + (1,) * (len(shape) - dim - 1))

    gain = one(*pieces[0])
    for cut in pieces[1:]:
        gain = gain * one(*cut)
    return gain


def bell_draw(key, dims, scale, bound, pieces=(), held_as=jnp.bfloat16):
    drawn = scale * jax.random.normal(key, dims, jnp.float32)
    if pieces:
        drawn = drawn * shard_levels(key, dims, pieces, -0.22, 0.18)
    return jnp.clip(drawn, -bound, bound).astype(held_as)


def setup_inputs(seed: int = 0) -> dict:
    keys = jax.random.split(jax.random.key(seed), 6)
    return {
        "residuals": bell_draw(keys[0], (2, ROWS), 1.0, 6.0, ((1, 512),), jnp.float32),
        "camera_jac": bell_draw(keys[1], (18, ROWS), 1.5, 9.0, ((1, 512),), jnp.float32),
        "point_jac": bell_draw(keys[2], (6, ROWS), 1.0, 6.0, ((1, 512),), jnp.float32),
        "obs_index": draw_obs_index(jax.random.fold_in(keys[5], 71), 0),
        "damping": jnp.clip(jnp.exp(math.log(4.0) - 2.0794415 * jax.random.uniform(keys[4], (TRACKS,), jnp.float32) ** shard_levels(keys[4], (TRACKS,), ((0, 128),), -0.2, 0.2)), 0.5, 4.0),
    }


HUBER_DELTA = 1.0
UPPER_PAIRS = ((0, 0), (0, 1), (0, 2), (1, 1), (1, 2), (2, 2))
DIAGONAL_MASK = (1.0, 0.0, 0.0, 1.0, 0.0, 1.0)

def huber_weights(residuals, alive_mask):
    magnitude = jnp.sqrt(residuals[0] * residuals[0] + residuals[1] * residuals[1])
    return alive_mask.astype(jnp.float32) * (HUBER_DELTA / jnp.maximum(magnitude, HUBER_DELTA))

def coupling(camera_jac, point_jac, weights):
    first = camera_jac[:9, None] * point_jac[None, :3]
    second = camera_jac[9:, None] * point_jac[None, 3:]
    joined = (first + second) * weights
    return joined.reshape((27,) + weights.shape)

def point_terms(point_jac, weights):
    return jnp.stack([weights * (point_jac[k] * point_jac[l] + point_jac[3 + k] * point_jac[3 + l]) for k, l in UPPER_PAIRS])

def point_inverse(points, damping):
    diagonal = jnp.asarray(DIAGONAL_MASK, dtype=jnp.float32)[:, None]
    full_block = points + diagonal * damping[None]
    a, b, c, d, e, f = (full_block[0], full_block[1], full_block[2], full_block[3], full_block[4], full_block[5])
    cofactor = jnp.stack([d * f - e * e, c * e - b * f, b * e - c * d, a * f - c * c, b * c - a * e, a * d - b * b])
    determinant = a * cofactor[0] + b * cofactor[1] + c * cofactor[2]
    scaled = cofactor / determinant
    entry_order = (0, 1, 2, 1, 3, 4, 2, 4, 5)
    return jnp.stack([scaled[i] for i in entry_order]).reshape((3, 3) + damping.shape)

def block_panels(couplings, visible_block, camera_position, offsets):
    block_match = (visible_block[None] == offsets[:, None, None]).astype(jnp.float32)
    position_equal = (camera_position[None] == jnp.arange(CAMERAS_PER_BLK, dtype=jnp.int32)[:, None, None]).astype(jnp.float32)
    selector = block_match[:, None] * position_equal[None]
    panels = jnp.einsum('misp,xsp->mixp', selector, couplings, precision=lax.Precision.HIGHEST)
    return panels.reshape((offsets.shape[0], TS, 3, couplings.shape[-1]))

def solve_panels(panels, inverse):
    return jnp.einsum('makp,klp->malp', panels, inverse, precision=lax.Precision.HIGHEST)

def tile_products(left_flat, right_flat):
    return lax.dot_general(left_flat, right_flat, (((1,), (1,)), ((), ())), precision=lax.Precision.HIGHEST)

def reference(residuals, camera_jac, point_jac, obs_index, damping):
    columns = jnp.arange(N_CAM, dtype=jnp.int32)[:, None] * (KC * TRK_DEV)
    offsets = jnp.arange(WIN, dtype=jnp.int32)
    row_block = offsets[:, None] + 0 * offsets[None, :]
    col_block = offsets[None, :] + 0 * offsets[:, None]
    owner_step = row_block // 2
    column_index = 2 * (row_block % 2) + col_block % 2
    slot_index = col_block // 2 - row_block // 2 + HOPS

    def pick(array, tile_strip):
        shaped = array.reshape((array.shape[0], N_TRK, N_CAM, N_TRK, SPR))
        taken = lax.dynamic_index_in_dim(shaped, tile_strip, 3, keepdims=False)
        return jnp.transpose(taken, (0, 2, 1, 3)).reshape((array.shape[0], N_CAM * N_TRK * SPR))

    def place(values, target):
        placed = jnp.zeros((values.shape[0], SLOTS * TRK_DEV), values.dtype).at[:, target].set(values)
        return placed.reshape((values.shape[0], SLOTS, TRK_DEV))

    def add_slab(summed, tile_strip):
        indices = pick(obs_index, tile_strip)
        target = (columns + indices[0].reshape((N_CAM, N_TRK * SPR))).reshape(-1)
        residual_slots = place(pick(residuals, tile_strip), target)
        camera_slots = place(pick(camera_jac, tile_strip), target)
        point_slots = place(pick(point_jac, tile_strip), target)
        index_positions = place(indices[1:], target)
        weights = huber_weights(residual_slots, index_positions[1])
        couplings = coupling(camera_slots, point_slots, weights)
        points = point_terms(point_slots, weights).sum(axis=1)
        slab_damping = lax.dynamic_slice_in_dim(damping, tile_strip * TRK_DEV, TRK_DEV)
        inverse = point_inverse(points, slab_damping)
        visible_block = jnp.mod(index_positions[0] // CAMERAS_PER_BLK - 2 * tile_strip, CAMERA_BLOCKS)
        camera_position = index_positions[0] % CAMERAS_PER_BLK
        panels = block_panels(couplings, visible_block, camera_position, offsets)
        left_panels = solve_panels(panels, inverse)
        product = tile_products(left_panels.reshape((WIN * TS, -1)), panels.reshape((WIN * TS, -1)))
        tiles = product.reshape((WIN, TS, WIN, TS)).transpose((0, 2, 1, 3)).reshape((WIN, WIN, TS * TS))
        owner = jnp.mod(tile_strip + owner_step, N_TRK)
        return (summed.at[owner, column_index, slot_index].add(tiles), None)
    initial = jnp.zeros((N_TRK, N_CAM, TILE_OWN, TS * TS), jnp.float32)
    summed, _ = lax.scan(add_slab, initial, jnp.arange(N_TRK, dtype=jnp.int32))
    return summed
```

```python
import jax
import jax.numpy as jnp
from jax import lax
from jax.sharding import PartitionSpec as P

CAMERAS_PER_BLK = 16
TS = 144
HOPS = 3


HUBER_DELTA = 1.0
UPPER_PAIRS = ((0, 0), (0, 1), (0, 2), (1, 1), (1, 2), (2, 2))


def from_behind(x, axis, by):
    size = lax.axis_size(axis)
    return lax.ppermute(x, axis, [(i, (i + by) % size) for i in range(size)])


def body(residuals, camera_jac, point_jac, obs_index, damping):
    strip_count = lax.axis_size("trk")
    tracks = damping.shape[0]
    rows = residuals.shape[1]
    per_dest = rows // strip_count
    fields = jnp.concatenate(
        [residuals, camera_jac, point_jac, obs_index.astype(jnp.float32)], axis=0
    )
    nf = fields.shape[0]
    send = fields.reshape((nf, strip_count, per_dest)).transpose((1, 0, 2))
    send = send.reshape((strip_count, nf * per_dest))
    got = lax.all_to_all(send, "trk", split_axis=0, concat_axis=0, tiled=True)
    got = got.reshape((strip_count, nf, per_dest)).transpose((1, 0, 2)).reshape((nf, rows))
    position = got[nf - 3].astype(jnp.int32)
    local_slots = rows // tracks
    onehot = (position[:, None] == jnp.arange(rows, dtype=jnp.int32)[None, :]).astype(jnp.float32)
    kept = jnp.concatenate([got[: nf - 3], got[nf - 2 :]], axis=0)
    placed = jnp.dot(kept, onehot, precision=lax.Precision.HIGHEST)
    gathered = lax.all_gather(placed, "cam", axis=1, tiled=False)
    n_cam = gathered.shape[1]
    slots = n_cam * local_slots
    g = gathered.reshape((kept.shape[0], slots, tracks))
    res = g[0:2]
    cj = g[2:20]
    pj = g[20:26]
    cam = g[26].astype(jnp.int32)
    alive = g[27]
    magnitude = jnp.sqrt(res[0] * res[0] + res[1] * res[1])
    w = alive * (HUBER_DELTA / jnp.maximum(magnitude, HUBER_DELTA))
    coup = (cj[:9, None] * pj[None, :3] + cj[9:, None] * pj[None, 3:]) * w
    terms = [
        (w * (pj[k] * pj[l] + pj[3 + k] * pj[3 + l])).sum(axis=0) for k, l in UPPER_PAIRS
    ]
    a, b, c, d, e, f = terms
    a = a + damping
    d = d + damping
    f = f + damping
    cof = [d * f - e * e, c * e - b * f, b * e - c * d, a * f - c * c, b * c - a * e, a * d - b * b]
    det = a * cof[0] + b * cof[1] + c * cof[2]
    sc = [x / det for x in cof]
    inv = [[sc[0], sc[1], sc[2]], [sc[1], sc[3], sc[4]], [sc[2], sc[4], sc[5]]]
    left = jnp.stack(
        [coup[:, 0] * inv[0][l] + coup[:, 1] * inv[1][l] + coup[:, 2] * inv[2][l] for l in range(3)],
        axis=1,
    )
    strip_index = lax.axis_index("trk")
    column = lax.axis_index("cam")
    visible = jnp.mod(cam // CAMERAS_PER_BLK - 2 * strip_index, 2 * strip_count)
    key = visible * CAMERAS_PER_BLK + cam % CAMERAS_PER_BLK
    owners = HOPS + 1
    grp = jnp.arange(owners * CAMERAS_PER_BLK, dtype=jnp.int32)
    base = (2 * (grp // CAMERAS_PER_BLK)) * CAMERAS_PER_BLK + grp % CAMERAS_PER_BLK
    key_left = base + (column // 2) * CAMERAS_PER_BLK
    key_right = base + (column % 2) * CAMERAS_PER_BLK
    sel_left = (key[None] == key_left[:, None, None]).astype(jnp.float32)
    sel_right = (key[None] == key_right[:, None, None]).astype(jnp.float32)
    pan_left = jnp.sum(sel_left[:, None, None] * left[None], axis=3)
    pan_right = jnp.sum(sel_right[:, None, None] * coup[None], axis=3)
    width = owners * TS
    left_flat = pan_left.reshape((width, 3 * tracks))
    right_flat = pan_right.reshape((width, 3 * tracks))
    product = lax.dot_general(
        left_flat, right_flat, (((1,), (1,)), ((), ())), precision=lax.Precision.HIGHEST
    )
    tiles = product.reshape((owners, TS, owners, TS)).transpose((0, 2, 1, 3))
    tiles = tiles.reshape((owners, owners, TS * TS))
    tile_count = 2 * HOPS + 1
    summed = jnp.zeros((tile_count, TS * TS), jnp.float32)
    for distance in range(owners - 1, 0, -1):
        arrived = from_behind(tiles[distance], "trk", distance)
        summed = summed.at[HOPS - distance : tile_count - distance].add(arrived)
    summed = summed.at[HOPS:tile_count].add(tiles[0])
    return summed.reshape((1, 1, tile_count, TS * TS))


def solution(mesh):
    placed = (
        P(None, ("trk", "cam")),
        P(None, ("trk", "cam")),
        P(None, ("trk", "cam")),
        P(None, ("trk", "cam")),
        P("trk"),
    )
    return jax.shard_map(
        body, mesh=mesh, in_specs=placed, out_specs=P("trk", "cam", None, None), check_vma=False
    )
```

```python
import jax
import jax.numpy as jnp
from jax import lax
from jax.sharding import PartitionSpec as P

CAMERAS_PER_BLK = 16
TS = 144
HOPS = 3


HUBER_DELTA = 1.0
UPPER_PAIRS = ((0, 0), (0, 1), (0, 2), (1, 1), (1, 2), (2, 2))


def from_behind(x, axis, by):
    size = lax.axis_size(axis)
    return lax.ppermute(x, axis, [(i, (i + by) % size) for i in range(size)])


def body(residuals, camera_jac, point_jac, obs_index, damping):
    strip_count = lax.axis_size("trk")
    tracks = damping.shape[0]
    rows = residuals.shape[1]
    per_dest = rows // strip_count
    fields = jnp.concatenate(
        [residuals, camera_jac, point_jac, obs_index.astype(jnp.float32)], axis=0
    )
    nf = fields.shape[0]
    send = fields.reshape((nf, strip_count, per_dest)).transpose((1, 0, 2))
    send = send.reshape((strip_count, nf * per_dest))
    got = lax.all_to_all(send, "trk", split_axis=0, concat_axis=0, tiled=True)
    got = got.reshape((strip_count, nf, per_dest)).transpose((1, 0, 2)).reshape((nf, rows))
    position = got[nf - 3].astype(jnp.int32)
    local_slots = rows // tracks
    onehot = (position[:, None] == jnp.arange(rows, dtype=jnp.int32)[None, :]).astype(jnp.float32)
    kept = jnp.concatenate([got[: nf - 3], got[nf - 2 :]], axis=0)
    placed = jnp.dot(kept, onehot, precision=lax.Precision.HIGHEST)
    gathered = lax.all_gather(placed, "cam", axis=1, tiled=False)
    n_cam = gathered.shape[1]
    slots = n_cam * local_slots
    g = gathered.reshape((kept.shape[0], slots, tracks))
    res = g[0:2]
    cj = g[2:20]
    pj = g[20:26]
    cam = g[26].astype(jnp.int32)
    alive = g[27]
    magnitude = jnp.sqrt(res[0] * res[0] + res[1] * res[1])
    w = alive * (HUBER_DELTA / jnp.maximum(magnitude, HUBER_DELTA))
    coup = (cj[:9, None] * pj[None, :3] + cj[9:, None] * pj[None, 3:]) * w
    terms = [
        (w * (pj[k] * pj[l] + pj[3 + k] * pj[3 + l])).sum(axis=0) for k, l in UPPER_PAIRS
    ]
    a, b, c, d, e, f = terms
    a = a + damping
    d = d + damping
    f = f + damping
    cof = [d * f - e * e, c * e - b * f, b * e - c * d, a * f - c * c, b * c - a * e, a * d - b * b]
    det = a * cof[0] + b * cof[1] + c * cof[2]
    sc = [x / det for x in cof]
    inv = [[sc[0], sc[1], sc[2]], [sc[1], sc[3], sc[4]], [sc[2], sc[4], sc[5]]]
    left = jnp.stack(
        [coup[:, 0] * inv[0][l] + coup[:, 1] * inv[1][l] + coup[:, 2] * inv[2][l] for l in range(3)],
        axis=1,
    )
    strip_index = lax.axis_index("trk")
    column = lax.axis_index("cam")
    visible = jnp.mod(cam // CAMERAS_PER_BLK - 2 * strip_index, 2 * strip_count)
    key = visible * CAMERAS_PER_BLK + cam % CAMERAS_PER_BLK
    owners = HOPS + 1
    grp = jnp.arange(owners * CAMERAS_PER_BLK, dtype=jnp.int32)
    base = (2 * (grp // CAMERAS_PER_BLK)) * CAMERAS_PER_BLK + grp % CAMERAS_PER_BLK
    key_left = base + (column // 2) * CAMERAS_PER_BLK
    key_right = base + (column % 2) * CAMERAS_PER_BLK
    sel_left = (key[None] == key_left[:, None, None]).astype(jnp.float32)
    sel_right = (key[None] == key_right[:, None, None]).astype(jnp.float32)
    left3 = left.transpose((0, 2, 1, 3)).reshape((9, slots, 3 * tracks))
    coup3 = coup.transpose((0, 2, 1, 3)).reshape((9, slots, 3 * tracks))
    key3 = jnp.tile(key, (1, 3))
    sel_left = (key3[None] == key_left[:, None, None]).astype(jnp.float32)
    sel_right = (key3[None] == key_right[:, None, None]).astype(jnp.float32)
    pan_left = jnp.sum(sel_left[None] * left3[:, None], axis=2)
    pan_right = jnp.sum(sel_right[None] * coup3[:, None], axis=2)
    width = owners * TS
    left_flat = pan_left.reshape((width, 3 * tracks))
    right_flat = pan_right.reshape((width, 3 * tracks))
    product = lax.dot_general(
        left_flat, right_flat, (((1,), (1,)), ((), ())), precision=lax.Precision.HIGH
    )
    tiles = product.reshape((9, owners, CAMERAS_PER_BLK, 9, owners, CAMERAS_PER_BLK))
    tiles = tiles.transpose((1, 4, 2, 0, 5, 3)).reshape((owners, owners, TS * TS))
    tile_count = 2 * HOPS + 1
    summed = jnp.pad(tiles[0], ((HOPS, 0), (0, 0)))
    for distance in range(owners - 1, 0, -1):
        arrived = from_behind(tiles[distance], "trk", distance)
        summed = summed + jnp.pad(arrived, ((HOPS - distance, distance), (0, 0)))
    return summed.reshape((1, 1, tile_count, TS * TS))


def solution(mesh):
    placed = (
        P(None, ("trk", "cam")),
        P(None, ("trk", "cam")),
        P(None, ("trk", "cam")),
        P(None, ("trk", "cam")),
        P("trk"),
    )
    return jax.shard_map(
        body, mesh=mesh, in_specs=placed, out_specs=P("trk", "cam", None, None), check_vma=False
    )
```

```python
import jax
import jax.numpy as jnp
from jax import lax
from jax.sharding import PartitionSpec as P

CAMERAS_PER_BLK = 16
TS = 144
HOPS = 3


HUBER_DELTA = 1.0
UPPER_PAIRS = ((0, 0), (0, 1), (0, 2), (1, 1), (1, 2), (2, 2))


def from_behind(x, axis, by):
    size = lax.axis_size(axis)
    return lax.ppermute(x, axis, [(i, (i + by) % size) for i in range(size)])


def body(residuals, camera_jac, point_jac, obs_index, damping):
    strip_count = lax.axis_size("trk")
    tracks = damping.shape[0]
    rows = residuals.shape[1]
    per_dest = rows // strip_count
    fields = jnp.concatenate(
        [residuals, camera_jac, point_jac, obs_index.astype(jnp.float32)], axis=0
    )
    nf = fields.shape[0]
    send = fields.reshape((nf, strip_count, per_dest)).transpose((1, 0, 2))
    send = send.reshape((strip_count, nf * per_dest))
    got = lax.all_to_all(send, "trk", split_axis=0, concat_axis=0, tiled=True)
    got = got.reshape((strip_count, nf, per_dest)).transpose((1, 0, 2)).reshape((nf, rows))
    position = got[nf - 3].astype(jnp.int32)
    local_slots = rows // tracks
    onehot = (position[:, None] == jnp.arange(rows, dtype=jnp.int32)[None, :]).astype(jnp.float32)
    kept = jnp.concatenate([got[: nf - 3], got[nf - 2 :]], axis=0)
    placed = jnp.dot(kept, onehot, precision=lax.Precision.HIGHEST)
    gathered = lax.all_gather(placed, "cam", axis=1, tiled=False)
    n_cam = gathered.shape[1]
    slots = n_cam * local_slots
    g = gathered.reshape((kept.shape[0], slots, tracks))
    res = g[0:2]
    cj = g[2:20]
    pj = g[20:26]
    cam = g[26].astype(jnp.int32)
    alive = g[27]
    magnitude = jnp.sqrt(res[0] * res[0] + res[1] * res[1])
    w = alive * (HUBER_DELTA / jnp.maximum(magnitude, HUBER_DELTA))
    coup = (cj[:9, None] * pj[None, :3] + cj[9:, None] * pj[None, 3:]) * w
    terms = [
        (w * (pj[k] * pj[l] + pj[3 + k] * pj[3 + l])).sum(axis=0) for k, l in UPPER_PAIRS
    ]
    a, b, c, d, e, f = terms
    a = a + damping
    d = d + damping
    f = f + damping
    cof = [d * f - e * e, c * e - b * f, b * e - c * d, a * f - c * c, b * c - a * e, a * d - b * b]
    det = a * cof[0] + b * cof[1] + c * cof[2]
    sc = [x / det for x in cof]
    inv = [[sc[0], sc[1], sc[2]], [sc[1], sc[3], sc[4]], [sc[2], sc[4], sc[5]]]
    left = jnp.stack(
        [coup[:, 0] * inv[0][l] + coup[:, 1] * inv[1][l] + coup[:, 2] * inv[2][l] for l in range(3)],
        axis=1,
    )
    strip_index = lax.axis_index("trk")
    column = lax.axis_index("cam")
    visible = jnp.mod(cam // CAMERAS_PER_BLK - 2 * strip_index, 2 * strip_count)
    key = visible * CAMERAS_PER_BLK + cam % CAMERAS_PER_BLK
    owners = HOPS + 1
    grp = jnp.arange(owners * CAMERAS_PER_BLK, dtype=jnp.int32)
    base = (2 * (grp // CAMERAS_PER_BLK)) * CAMERAS_PER_BLK + grp % CAMERAS_PER_BLK
    key_left = base + (column // 2) * CAMERAS_PER_BLK
    key_right = base + (column % 2) * CAMERAS_PER_BLK
    left3 = left.transpose((0, 2, 1, 3)).reshape((9, slots, 3 * tracks))
    coup3 = coup.transpose((0, 2, 1, 3)).reshape((9, slots, 3 * tracks))
    key3 = jnp.tile(key, (1, 3))
    groups = owners * CAMERAS_PER_BLK
    width = owners * TS
    full = (groups, 9, slots, 3 * tracks)

    def panel(keys, values):
        sel = (key3[None] == keys[:, None, None]).astype(jnp.float32)
        sel = jnp.broadcast_to(sel[:, None], full).reshape((width, slots, 3 * tracks))
        vals = jnp.broadcast_to(values[None], full).reshape((width, slots, 3 * tracks))
        return jnp.sum(sel * vals, axis=1)

    left_flat = panel(key_left, left3)
    right_flat = panel(key_right, coup3)
    product = lax.dot_general(
        left_flat, right_flat, (((1,), (1,)), ((), ())), precision=lax.Precision.HIGH
    )
    tiles = product.reshape((owners, TS, owners, TS)).transpose((0, 2, 1, 3))
    tiles = tiles.reshape((owners, owners, TS * TS))
    tile_count = 2 * HOPS + 1
    summed = jnp.pad(tiles[0], ((HOPS, 0), (0, 0)))
    for distance in range(owners - 1, 0, -1):
        arrived = from_behind(tiles[distance], "trk", distance)
        summed = summed + jnp.pad(arrived, ((HOPS - distance, distance), (0, 0)))
    return summed.reshape((1, 1, tile_count, TS * TS))


def solution(mesh):
    placed = (
        P(None, ("trk", "cam")),
        P(None, ("trk", "cam")),
        P(None, ("trk", "cam")),
        P(None, ("trk", "cam")),
        P("trk"),
    )
    return jax.shard_map(
        body, mesh=mesh, in_specs=placed, out_specs=P("trk", "cam", None, None), check_vma=False
    )
```

```python
import jax
import jax.numpy as jnp
from jax import lax
from jax.sharding import PartitionSpec as P

CAMERAS_PER_BLK = 16
TS = 144
HOPS = 3
SHIFT = 2
CAM_BY_ALL_TO_ALL = True


HUBER_DELTA = 1.0
UPPER_PAIRS = ((0, 0), (0, 1), (0, 2), (1, 1), (1, 2), (2, 2))


def from_behind(x, axis, by):
    size = lax.axis_size(axis)
    return lax.ppermute(x, axis, [(i, (i + by) % size) for i in range(size)])


def body(residuals, camera_jac, point_jac, obs_index, damping):
    strip_count = lax.axis_size("trk")
    tracks = damping.shape[0]
    rows = residuals.shape[1]
    per_dest = rows // strip_count
    fields = jnp.concatenate(
        [residuals, camera_jac, point_jac, obs_index.astype(jnp.float32)], axis=0
    )
    nf = fields.shape[0]
    send = fields.reshape((nf, strip_count, per_dest)).transpose((1, 0, 2))
    send = send.reshape((strip_count, nf * per_dest))
    send = jnp.roll(send, SHIFT, axis=0)
    got = lax.all_to_all(send, "trk", split_axis=0, concat_axis=0, tiled=True)
    got = got.reshape((strip_count, nf, per_dest)).transpose((1, 0, 2)).reshape((nf, rows))
    position = got[nf - 3].astype(jnp.int32)
    local_slots = rows // tracks
    onehot = (position[:, None] == jnp.arange(rows, dtype=jnp.int32)[None, :]).astype(jnp.float32)
    kept = jnp.concatenate([got[: nf - 3], got[nf - 2 :]], axis=0)
    placed = jnp.dot(kept, onehot, precision=lax.Precision.HIGHEST)
    if CAM_BY_ALL_TO_ALL:
        n_cam = lax.axis_size("cam")
        copies = jnp.broadcast_to(placed[None], (n_cam,) + placed.shape)
        gathered = lax.all_to_all(copies, "cam", 0, 0, tiled=True).transpose((1, 0, 2))
    else:
        gathered = lax.all_gather(placed, "cam", axis=1, tiled=False)
        n_cam = gathered.shape[1]
    damping = from_behind(damping, "trk", SHIFT)
    slots = n_cam * local_slots
    g = gathered.reshape((kept.shape[0], slots, tracks))
    res = g[0:2]
    cj = g[2:20]
    pj = g[20:26]
    cam = g[26].astype(jnp.int32)
    alive = g[27]
    magnitude = jnp.sqrt(res[0] * res[0] + res[1] * res[1])
    w = alive * (HUBER_DELTA / jnp.maximum(magnitude, HUBER_DELTA))
    coup = (cj[:9, None] * pj[None, :3] + cj[9:, None] * pj[None, 3:]) * w
    terms = [
        (w * (pj[k] * pj[l] + pj[3 + k] * pj[3 + l])).sum(axis=0) for k, l in UPPER_PAIRS
    ]
    a, b, c, d, e, f = terms
    a = a + damping
    d = d + damping
    f = f + damping
    cof = [d * f - e * e, c * e - b * f, b * e - c * d, a * f - c * c, b * c - a * e, a * d - b * b]
    det = a * cof[0] + b * cof[1] + c * cof[2]
    sc = [x / det for x in cof]
    inv = [[sc[0], sc[1], sc[2]], [sc[1], sc[3], sc[4]], [sc[2], sc[4], sc[5]]]
    left = jnp.stack(
        [coup[:, 0] * inv[0][l] + coup[:, 1] * inv[1][l] + coup[:, 2] * inv[2][l] for l in range(3)],
        axis=1,
    )
    strip_index = jnp.mod(lax.axis_index("trk") - SHIFT, strip_count)
    column = lax.axis_index("cam")
    visible = jnp.mod(cam // CAMERAS_PER_BLK - 2 * strip_index, 2 * strip_count)
    key = visible * CAMERAS_PER_BLK + cam % CAMERAS_PER_BLK
    owners = HOPS + 1
    grp = jnp.arange(owners * CAMERAS_PER_BLK, dtype=jnp.int32)
    base = (2 * (grp // CAMERAS_PER_BLK)) * CAMERAS_PER_BLK + grp % CAMERAS_PER_BLK
    key_left = base + (column // 2) * CAMERAS_PER_BLK
    key_right = base + (column % 2) * CAMERAS_PER_BLK
    left3 = left.transpose((0, 2, 1, 3)).reshape((9, slots, 3 * tracks))
    coup3 = coup.transpose((0, 2, 1, 3)).reshape((9, slots, 3 * tracks))
    key3 = jnp.tile(key, (1, 3))
    groups = owners * CAMERAS_PER_BLK
    width = owners * TS
    full = (groups, 9, slots, 3 * tracks)

    def panel(keys, values):
        sel = (key3[None] == keys[:, None, None]).astype(jnp.float32)
        sel = jnp.broadcast_to(sel[:, None], full).reshape((width, slots, 3 * tracks))
        vals = jnp.broadcast_to(values[None], full).reshape((width, slots, 3 * tracks))
        return jnp.sum(sel * vals, axis=1)

    left_flat = panel(key_left, left3)
    right_flat = panel(key_right, coup3)
    product = lax.dot_general(
        left_flat, right_flat, (((1,), (1,)), ((), ())), precision=lax.Precision.HIGH
    )
    tiles = product.reshape((owners, TS, owners, TS)).transpose((0, 2, 1, 3))
    tiles = tiles.reshape((owners, owners, TS * TS))
    tile_count = 2 * HOPS + 1
    summed = jnp.zeros((tile_count, TS * TS), jnp.float32)
    for distance in range(owners - 1, -1, -1):
        by = distance - SHIFT
        arrived = tiles[distance] if by == 0 else from_behind(tiles[distance], "trk", by)
        summed = summed + jnp.pad(arrived, ((HOPS - distance, distance), (0, 0)))
    return summed.reshape((1, 1, tile_count, TS * TS))


def solution(mesh):
    placed = (
        P(None, ("trk", "cam")),
        P(None, ("trk", "cam")),
        P(None, ("trk", "cam")),
        P(None, ("trk", "cam")),
        P("trk"),
    )
    return jax.shard_map(
        body, mesh=mesh, in_specs=placed, out_specs=P("trk", "cam", None, None), check_vma=False
    )
```

```python
import jax
import jax.numpy as jnp
from jax import lax
from jax.sharding import PartitionSpec as P

CAMERAS_PER_BLK = 16
TS = 144
HOPS = 3
SHIFT = 2
CAM_BY_ALL_TO_ALL = True


HUBER_DELTA = 1.0
UPPER_PAIRS = ((0, 0), (0, 1), (0, 2), (1, 1), (1, 2), (2, 2))


def from_behind(x, axis, by):
    size = lax.axis_size(axis)
    return lax.ppermute(x, axis, [(i, (i + by) % size) for i in range(size)])


def body(residuals, camera_jac, point_jac, obs_index, damping):
    strip_count = lax.axis_size("trk")
    tracks = damping.shape[0]
    rows = residuals.shape[1]
    per_dest = rows // strip_count
    fields = jnp.concatenate(
        [residuals, camera_jac, point_jac, obs_index.astype(jnp.float32)], axis=0
    )
    nf = fields.shape[0]
    send = fields.reshape((nf, strip_count, per_dest)).transpose((1, 0, 2))
    send = send.reshape((strip_count, nf * per_dest))
    send = jnp.roll(send, SHIFT, axis=0)
    got = lax.all_to_all(send, "trk", split_axis=0, concat_axis=0, tiled=True)
    got = got.reshape((strip_count, nf, per_dest)).transpose((1, 0, 2)).reshape((nf, rows))
    position = got[nf - 3].astype(jnp.int32)
    local_slots = rows // tracks
    onehot = (position[:, None] == jnp.arange(rows, dtype=jnp.int32)[None, :]).astype(jnp.float32)
    kept = jnp.concatenate([got[: nf - 3], got[nf - 2 :]], axis=0)
    placed = jnp.dot(kept, onehot, precision=lax.Precision.HIGHEST)
    if CAM_BY_ALL_TO_ALL:
        n_cam = lax.axis_size("cam")
        copies = jnp.broadcast_to(placed[None], (n_cam,) + placed.shape)
        gathered = lax.all_to_all(copies, "cam", 0, 0, tiled=True).transpose((1, 0, 2))
    else:
        gathered = lax.all_gather(placed, "cam", axis=1, tiled=False)
        n_cam = gathered.shape[1]
    damping = from_behind(damping, "trk", SHIFT)
    slots = n_cam * local_slots
    g = gathered.reshape((kept.shape[0], slots, tracks))
    res = g[0:2]
    cj = g[2:20]
    pj = g[20:26]
    cam = g[26].astype(jnp.int32)
    alive = g[27]
    magnitude = jnp.sqrt(res[0] * res[0] + res[1] * res[1])
    w = alive * (HUBER_DELTA / jnp.maximum(magnitude, HUBER_DELTA))
    coup = (cj[:9, None] * pj[None, :3] + cj[9:, None] * pj[None, 3:]) * w
    terms = [
        (w * (pj[k] * pj[l] + pj[3 + k] * pj[3 + l])).sum(axis=0) for k, l in UPPER_PAIRS
    ]
    a, b, c, d, e, f = terms
    a = a + damping
    d = d + damping
    f = f + damping
    cof = [d * f - e * e, c * e - b * f, b * e - c * d, a * f - c * c, b * c - a * e, a * d - b * b]
    det = a * cof[0] + b * cof[1] + c * cof[2]
    sc = [x / det for x in cof]
    inv = [[sc[0], sc[1], sc[2]], [sc[1], sc[3], sc[4]], [sc[2], sc[4], sc[5]]]
    left = jnp.stack(
        [coup[:, 0] * inv[0][l] + coup[:, 1] * inv[1][l] + coup[:, 2] * inv[2][l] for l in range(3)],
        axis=1,
    )
    strip_index = jnp.mod(lax.axis_index("trk") - SHIFT, strip_count)
    column = lax.axis_index("cam")
    visible = jnp.mod(cam // CAMERAS_PER_BLK - 2 * strip_index, 2 * strip_count)
    key = visible * CAMERAS_PER_BLK + cam % CAMERAS_PER_BLK
    owners = HOPS + 1
    grp = jnp.arange(owners * CAMERAS_PER_BLK, dtype=jnp.int32)
    base = (2 * (grp // CAMERAS_PER_BLK)) * CAMERAS_PER_BLK + grp % CAMERAS_PER_BLK
    key_left = base + (column // 2) * CAMERAS_PER_BLK
    key_right = base + (column % 2) * CAMERAS_PER_BLK
    left3 = left.transpose((0, 2, 1, 3)).reshape((9, slots, 3 * tracks))
    coup3 = coup.transpose((0, 2, 1, 3)).reshape((9, slots, 3 * tracks))
    key3 = jnp.tile(key, (1, 3))
    groups = owners * CAMERAS_PER_BLK
    width = owners * TS

    def panel(keys, values):
        sel = (key3[None] == keys[:, None, None]).astype(jnp.float32)
        return jnp.sum(sel[None] * values[:, None], axis=2).reshape((width, 3 * tracks))

    new_row = jnp.arange(width, dtype=jnp.int32)
    old_row = (new_row % 9) * groups + new_row // 9
    reorder = (old_row[:, None] == jnp.arange(width, dtype=jnp.int32)[None, :]).astype(jnp.float32)
    left_flat = jnp.dot(reorder, panel(key_left, left3), precision=lax.Precision.HIGH)
    right_flat = jnp.dot(reorder, panel(key_right, coup3), precision=lax.Precision.HIGH)
    product = lax.dot_general(
        left_flat, right_flat, (((1,), (1,)), ((), ())), precision=lax.Precision.HIGH
    )
    tiles = product.reshape((owners, TS, owners, TS)).transpose((0, 2, 1, 3))
    tiles = tiles.reshape((owners, owners, TS * TS))
    tile_count = 2 * HOPS + 1
    summed = jnp.zeros((tile_count, TS * TS), jnp.float32)
    for distance in range(owners - 1, -1, -1):
        by = distance - SHIFT
        arrived = tiles[distance] if by == 0 else from_behind(tiles[distance], "trk", by)
        summed = summed + jnp.pad(arrived, ((HOPS - distance, distance), (0, 0)))
    return summed.reshape((1, 1, tile_count, TS * TS))


def solution(mesh):
    placed = (
        P(None, ("trk", "cam")),
        P(None, ("trk", "cam")),
        P(None, ("trk", "cam")),
        P(None, ("trk", "cam")),
        P("trk"),
    )
    return jax.shard_map(
        body, mesh=mesh, in_specs=placed, out_specs=P("trk", "cam", None, None), check_vma=False
    )
```

```python
import jax
import jax.numpy as jnp
from jax import lax
from jax.sharding import PartitionSpec as P

CAMERAS_PER_BLK = 16
TS = 144
HOPS = 3
SHIFT = 2
CAM_BY_ALL_TO_ALL = True


HUBER_DELTA = 1.0
UPPER_PAIRS = ((0, 0), (0, 1), (0, 2), (1, 1), (1, 2), (2, 2))


def from_behind(x, axis, by):
    size = lax.axis_size(axis)
    return lax.ppermute(x, axis, [(i, (i + by) % size) for i in range(size)])


def body(residuals, camera_jac, point_jac, obs_index, damping):
    strip_count = lax.axis_size("trk")
    tracks = damping.shape[0]
    rows = residuals.shape[1]
    per_dest = rows // strip_count
    fields = jnp.concatenate(
        [residuals, camera_jac, point_jac, obs_index.astype(jnp.float32)], axis=0
    )
    nf = fields.shape[0]
    send = fields.reshape((nf, strip_count, per_dest)).transpose((1, 0, 2))
    send = send.reshape((strip_count, nf * per_dest))
    send = jnp.roll(send, SHIFT, axis=0)
    got = lax.all_to_all(send, "trk", split_axis=0, concat_axis=0, tiled=True)
    got = got.reshape((strip_count, nf, per_dest)).transpose((1, 0, 2)).reshape((nf, rows))
    position = got[nf - 3].astype(jnp.int32)
    local_slots = rows // tracks
    onehot = (position[:, None] == jnp.arange(rows, dtype=jnp.int32)[None, :]).astype(jnp.float32)
    kept = jnp.concatenate([got[: nf - 3], got[nf - 2 :]], axis=0)
    placed = jnp.dot(kept, onehot, precision=lax.Precision.HIGHEST)
    if CAM_BY_ALL_TO_ALL:
        n_cam = lax.axis_size("cam")
        copies = jnp.broadcast_to(placed[None], (n_cam,) + placed.shape)
        gathered = lax.all_to_all(copies, "cam", 0, 0, tiled=True).transpose((1, 0, 2))
    else:
        gathered = lax.all_gather(placed, "cam", axis=1, tiled=False)
        n_cam = gathered.shape[1]
    damping = from_behind(damping, "trk", SHIFT)
    slots = n_cam * local_slots
    g = gathered.reshape((kept.shape[0], slots, tracks))
    res = g[0:2]
    cj = g[2:20]
    pj = g[20:26]
    cam = g[26].astype(jnp.int32)
    alive = g[27]
    magnitude = jnp.sqrt(res[0] * res[0] + res[1] * res[1])
    w = alive * (HUBER_DELTA / jnp.maximum(magnitude, HUBER_DELTA))
    coup = (cj[:9, None] * pj[None, :3] + cj[9:, None] * pj[None, 3:]) * w
    terms = [
        (w * (pj[k] * pj[l] + pj[3 + k] * pj[3 + l])).sum(axis=0) for k, l in UPPER_PAIRS
    ]
    a, b, c, d, e, f = terms
    a = a + damping
    d = d + damping
    f = f + damping
    cof = [d * f - e * e, c * e - b * f, b * e - c * d, a * f - c * c, b * c - a * e, a * d - b * b]
    det = a * cof[0] + b * cof[1] + c * cof[2]
    sc = [x / det for x in cof]
    inv = [[sc[0], sc[1], sc[2]], [sc[1], sc[3], sc[4]], [sc[2], sc[4], sc[5]]]
    left = jnp.stack(
        [coup[:, 0] * inv[0][l] + coup[:, 1] * inv[1][l] + coup[:, 2] * inv[2][l] for l in range(3)],
        axis=1,
    )
    strip_index = jnp.mod(lax.axis_index("trk") - SHIFT, strip_count)
    column = lax.axis_index("cam")
    visible = jnp.mod(cam // CAMERAS_PER_BLK - 2 * strip_index, 2 * strip_count)
    key = visible * CAMERAS_PER_BLK + cam % CAMERAS_PER_BLK
    owners = HOPS + 1
    grp = jnp.arange(owners * CAMERAS_PER_BLK, dtype=jnp.int32)
    base = (2 * (grp // CAMERAS_PER_BLK)) * CAMERAS_PER_BLK + grp % CAMERAS_PER_BLK
    key_left = base + (column // 2) * CAMERAS_PER_BLK
    key_right = base + (column % 2) * CAMERAS_PER_BLK
    left3 = left.transpose((0, 2, 1, 3)).reshape((9, slots, 3 * tracks))
    coup3 = coup.transpose((0, 2, 1, 3)).reshape((9, slots, 3 * tracks))
    key3 = jnp.tile(key, (1, 3))
    groups = owners * CAMERAS_PER_BLK
    width = owners * TS

    def panel(keys, values):
        sel = (key3[None] == keys[:, None, None]).astype(jnp.float32)
        return jnp.sum(sel[None] * values[:, None], axis=2).reshape((width, 3 * tracks))

    new_row = jnp.arange(width, dtype=jnp.int32)
    old_row = (new_row % 9) * groups + new_row // 9
    reorder = (old_row[:, None] == jnp.arange(width, dtype=jnp.int32)[None, :]).astype(jnp.float32)
    left_flat = jnp.dot(reorder, panel(key_left, left3), precision=lax.Precision.HIGH)
    right_flat = jnp.dot(reorder, panel(key_right, coup3), precision=lax.Precision.HIGH)
    left4 = left_flat.reshape((owners, TS, 3 * tracks))
    right4 = right_flat.reshape((owners, TS, 3 * tracks))
    tiles = jnp.einsum("kic,mjc->kmij", left4, right4, precision=lax.Precision.HIGH)
    tiles = tiles.reshape((owners, owners, TS * TS))
    tile_count = 2 * HOPS + 1
    summed = jnp.zeros((tile_count, TS * TS), jnp.float32)
    for distance in range(owners - 1, -1, -1):
        by = distance - SHIFT
        arrived = tiles[distance] if by == 0 else from_behind(tiles[distance], "trk", by)
        summed = summed + jnp.pad(arrived, ((HOPS - distance, distance), (0, 0)))
    return summed.reshape((1, 1, tile_count, TS * TS))


def solution(mesh):
    placed = (
        P(None, ("trk", "cam")),
        P(None, ("trk", "cam")),
        P(None, ("trk", "cam")),
        P(None, ("trk", "cam")),
        P("trk"),
    )
    return jax.shard_map(
        body, mesh=mesh, in_specs=placed, out_specs=P("trk", "cam", None, None), check_vma=False
    )
```

```python
import jax
import jax.numpy as jnp
from jax import lax
from jax.sharding import PartitionSpec as P

CAMERAS_PER_BLK = 16
TS = 144
HOPS = 3
SHIFT = 2
CAM_BY_ALL_TO_ALL = True


HUBER_DELTA = 1.0
UPPER_PAIRS = ((0, 0), (0, 1), (0, 2), (1, 1), (1, 2), (2, 2))


def from_behind(x, axis, by):
    size = lax.axis_size(axis)
    return lax.ppermute(x, axis, [(i, (i + by) % size) for i in range(size)])


def body(residuals, camera_jac, point_jac, obs_index, damping):
    strip_count = lax.axis_size("trk")
    tracks = damping.shape[0]
    rows = residuals.shape[1]
    per_dest = rows // strip_count
    fields = jnp.concatenate(
        [residuals, camera_jac, point_jac, obs_index.astype(jnp.float32)], axis=0
    )
    nf = fields.shape[0]
    send = fields.reshape((nf, strip_count, per_dest)).transpose((1, 0, 2))
    send = send.reshape((strip_count, nf * per_dest))
    send = jnp.roll(send, SHIFT, axis=0)
    got = lax.all_to_all(send, "trk", split_axis=0, concat_axis=0, tiled=True)
    got = got.reshape((strip_count, nf, per_dest)).transpose((1, 0, 2)).reshape((nf, rows))
    position = got[nf - 3].astype(jnp.int32)
    local_slots = rows // tracks
    onehot = (position[:, None] == jnp.arange(rows, dtype=jnp.int32)[None, :]).astype(jnp.float32)
    kept = jnp.concatenate([got[: nf - 3], got[nf - 2 :]], axis=0)
    placed = jnp.dot(kept, onehot, precision=lax.Precision.HIGHEST)
    if CAM_BY_ALL_TO_ALL:
        n_cam = lax.axis_size("cam")
        copies = jnp.broadcast_to(placed[None], (n_cam,) + placed.shape)
        gathered = lax.all_to_all(copies, "cam", 0, 0, tiled=True).transpose((1, 0, 2))
    else:
        gathered = lax.all_gather(placed, "cam", axis=1, tiled=False)
        n_cam = gathered.shape[1]
    damping = from_behind(damping, "trk", SHIFT)
    slots = n_cam * local_slots
    g = gathered.reshape((kept.shape[0], slots, tracks))
    res = g[0:2]
    cj = g[2:20]
    pj = g[20:26]
    cam = g[26].astype(jnp.int32)
    alive = g[27]
    magnitude = jnp.sqrt(res[0] * res[0] + res[1] * res[1])
    w = alive * (HUBER_DELTA / jnp.maximum(magnitude, HUBER_DELTA))
    coup = (cj[:9, None] * pj[None, :3] + cj[9:, None] * pj[None, 3:]) * w
    terms = [
        (w * (pj[k] * pj[l] + pj[3 + k] * pj[3 + l])).sum(axis=0) for k, l in UPPER_PAIRS
    ]
    a, b, c, d, e, f = terms
    a = a + damping
    d = d + damping
    f = f + damping
    cof = [d * f - e * e, c * e - b * f, b * e - c * d, a * f - c * c, b * c - a * e, a * d - b * b]
    det = a * cof[0] + b * cof[1] + c * cof[2]
    sc = [x / det for x in cof]
    inv = [[sc[0], sc[1], sc[2]], [sc[1], sc[3], sc[4]], [sc[2], sc[4], sc[5]]]
    left = jnp.stack(
        [coup[:, 0] * inv[0][l] + coup[:, 1] * inv[1][l] + coup[:, 2] * inv[2][l] for l in range(3)],
        axis=1,
    )
    strip_index = jnp.mod(lax.axis_index("trk") - SHIFT, strip_count)
    column = lax.axis_index("cam")
    visible = jnp.mod(cam // CAMERAS_PER_BLK - 2 * strip_index, 2 * strip_count)
    key = visible * CAMERAS_PER_BLK + cam % CAMERAS_PER_BLK
    owners = HOPS + 1
    grp = jnp.arange(owners * CAMERAS_PER_BLK, dtype=jnp.int32)
    base = (2 * (grp // CAMERAS_PER_BLK)) * CAMERAS_PER_BLK + grp % CAMERAS_PER_BLK
    key_left = base + (column // 2) * CAMERAS_PER_BLK
    key_right = base + (column % 2) * CAMERAS_PER_BLK
    left3 = left.transpose((0, 2, 1, 3)).reshape((9, slots, 3 * tracks))
    coup3 = coup.transpose((0, 2, 1, 3)).reshape((9, slots, 3 * tracks))
    key3 = jnp.tile(key, (1, 3))
    groups = owners * CAMERAS_PER_BLK
    width = owners * TS
    full = (groups, 9, slots, 3 * tracks)

    def panel(keys, values):
        sel = (key3[None] == keys[:, None, None]).astype(jnp.float32)
        sel = jnp.broadcast_to(sel[:, None], full).reshape((width, slots, 3 * tracks))
        vals = jnp.broadcast_to(values[None], full).reshape((width, slots, 3 * tracks))
        return jnp.sum(sel * vals, axis=1)

    left_flat = panel(key_left, left3)
    right_flat = panel(key_right, coup3)

    def owner_rows(distance):
        rows_k = left_flat[distance * TS : (distance + 1) * TS]
        product = lax.dot_general(
            rows_k, right_flat, (((1,), (1,)), ((), ())), precision=lax.Precision.HIGH
        )
        return product.reshape((TS, owners, TS)).transpose((1, 0, 2)).reshape((owners, TS * TS))

    tile_count = 2 * HOPS + 1
    summed = jnp.zeros((tile_count, TS * TS), jnp.float32)
    for distance in sorted(range(owners), key=lambda k: (k == SHIFT, -k)):
        by = distance - SHIFT
        rows_k = owner_rows(distance)
        arrived = rows_k if by == 0 else from_behind(rows_k, "trk", by)
        summed = summed + jnp.pad(arrived, ((HOPS - distance, distance), (0, 0)))
    return summed.reshape((1, 1, tile_count, TS * TS))


def solution(mesh):
    placed = (
        P(None, ("trk", "cam")),
        P(None, ("trk", "cam")),
        P(None, ("trk", "cam")),
        P(None, ("trk", "cam")),
        P("trk"),
    )
    return jax.shard_map(
        body, mesh=mesh, in_specs=placed, out_specs=P("trk", "cam", None, None), check_vma=False
    )
```

```python
import jax
import jax.numpy as jnp
from jax import lax
from jax.sharding import PartitionSpec as P

CAMERAS_PER_BLK = 16
TS = 144
HOPS = 3
SHIFT = 2
CAM_BY_ALL_TO_ALL = True


HUBER_DELTA = 1.0
UPPER_PAIRS = ((0, 0), (0, 1), (0, 2), (1, 1), (1, 2), (2, 2))


def from_behind(x, axis, by):
    size = lax.axis_size(axis)
    return lax.ppermute(x, axis, [(i, (i + by) % size) for i in range(size)])


def body(residuals, camera_jac, point_jac, obs_index, damping):
    strip_count = lax.axis_size("trk")
    tracks = damping.shape[0]
    rows = residuals.shape[1]
    per_dest = rows // strip_count
    magnitude = jnp.sqrt(residuals[0] * residuals[0] + residuals[1] * residuals[1])
    weight = obs_index[2].astype(jnp.float32) * (HUBER_DELTA / jnp.maximum(magnitude, HUBER_DELTA))
    fields = jnp.concatenate(
        [camera_jac, point_jac, weight[None], obs_index[:2].astype(jnp.float32)], axis=0
    )
    nf = fields.shape[0]
    send = fields.reshape((nf, strip_count, per_dest)).transpose((1, 0, 2))
    send = send.reshape((strip_count, nf * per_dest))
    send = jnp.roll(send, SHIFT, axis=0)
    got = lax.all_to_all(send, "trk", split_axis=0, concat_axis=0, tiled=True)
    got = got.reshape((strip_count, nf, per_dest)).transpose((1, 0, 2)).reshape((nf, rows))
    position = got[nf - 2].astype(jnp.int32)
    local_slots = rows // tracks
    onehot = (position[:, None] == jnp.arange(rows, dtype=jnp.int32)[None, :]).astype(jnp.float32)
    kept = jnp.concatenate([got[: nf - 2], got[nf - 1 :]], axis=0)
    placed = jnp.dot(kept, onehot, precision=lax.Precision.HIGHEST)
    if CAM_BY_ALL_TO_ALL:
        n_cam = lax.axis_size("cam")
        copies = jnp.broadcast_to(placed[None], (n_cam,) + placed.shape)
        gathered = lax.all_to_all(copies, "cam", 0, 0, tiled=True).transpose((1, 0, 2))
    else:
        gathered = lax.all_gather(placed, "cam", axis=1, tiled=False)
        n_cam = gathered.shape[1]
    damping = from_behind(damping, "trk", SHIFT)
    slots = n_cam * local_slots
    g = gathered.reshape((kept.shape[0], slots, tracks))
    cj = g[0:18]
    pj = g[18:24]
    w = g[24]
    cam = g[25].astype(jnp.int32)
    coup = (cj[:9, None] * pj[None, :3] + cj[9:, None] * pj[None, 3:]) * w
    terms = [
        (w * (pj[k] * pj[l] + pj[3 + k] * pj[3 + l])).sum(axis=0) for k, l in UPPER_PAIRS
    ]
    a, b, c, d, e, f = terms
    a = a + damping
    d = d + damping
    f = f + damping
    cof = [d * f - e * e, c * e - b * f, b * e - c * d, a * f - c * c, b * c - a * e, a * d - b * b]
    det = a * cof[0] + b * cof[1] + c * cof[2]
    sc = [x / det for x in cof]
    inv = [[sc[0], sc[1], sc[2]], [sc[1], sc[3], sc[4]], [sc[2], sc[4], sc[5]]]
    left = jnp.stack(
        [coup[:, 0] * inv[0][l] + coup[:, 1] * inv[1][l] + coup[:, 2] * inv[2][l] for l in range(3)],
        axis=1,
    )
    strip_index = jnp.mod(lax.axis_index("trk") - SHIFT, strip_count)
    column = lax.axis_index("cam")
    visible = jnp.mod(cam // CAMERAS_PER_BLK - 2 * strip_index, 2 * strip_count)
    key = visible * CAMERAS_PER_BLK + cam % CAMERAS_PER_BLK
    owners = HOPS + 1
    grp = jnp.arange(owners * CAMERAS_PER_BLK, dtype=jnp.int32)
    base = (2 * (grp // CAMERAS_PER_BLK)) * CAMERAS_PER_BLK + grp % CAMERAS_PER_BLK
    key_left = base + (column // 2) * CAMERAS_PER_BLK
    key_right = base + (column % 2) * CAMERAS_PER_BLK
    left3 = left.transpose((0, 2, 1, 3)).reshape((9, slots, 3 * tracks))
    coup3 = coup.transpose((0, 2, 1, 3)).reshape((9, slots, 3 * tracks))
    key3 = jnp.tile(key, (1, 3))
    groups = owners * CAMERAS_PER_BLK
    width = owners * TS
    full = (groups, 9, slots, 3 * tracks)

    def panel(keys, values):
        sel = (key3[None] == keys[:, None, None]).astype(jnp.float32)
        sel = jnp.broadcast_to(sel[:, None], full).reshape((width, slots, 3 * tracks))
        vals = jnp.broadcast_to(values[None], full).reshape((width, slots, 3 * tracks))
        return jnp.sum(sel * vals, axis=1)

    left_flat = panel(key_left, left3)
    right_flat = panel(key_right, coup3)
    product = lax.dot_general(
        left_flat, right_flat, (((1,), (1,)), ((), ())), precision=lax.Precision.HIGH
    )
    tiles = product.reshape((owners, TS, owners, TS)).transpose((0, 2, 1, 3))
    tiles = tiles.reshape((owners, owners, TS * TS))
    tile_count = 2 * HOPS + 1
    summed = jnp.zeros((tile_count, TS * TS), jnp.float32)
    for distance in range(owners - 1, -1, -1):
        by = distance - SHIFT
        arrived = tiles[distance] if by == 0 else from_behind(tiles[distance], "trk", by)
        summed = summed + jnp.pad(arrived, ((HOPS - distance, distance), (0, 0)))
    return summed.reshape((1, 1, tile_count, TS * TS))


def solution(mesh):
    placed = (
        P(None, ("trk", "cam")),
        P(None, ("trk", "cam")),
        P(None, ("trk", "cam")),
        P(None, ("trk", "cam")),
        P("trk"),
    )
    return jax.shard_map(
        body, mesh=mesh, in_specs=placed, out_specs=P("trk", "cam", None, None), check_vma=False
    )
```

```python
import jax
import jax.numpy as jnp
from jax import lax
from jax.sharding import PartitionSpec as P

CAMERAS_PER_BLK = 16
TS = 144
HOPS = 3
SHIFT = 2
CAM_BY_ALL_TO_ALL = True


HUBER_DELTA = 1.0
UPPER_PAIRS = ((0, 0), (0, 1), (0, 2), (1, 1), (1, 2), (2, 2))


def from_behind(x, axis, by):
    size = lax.axis_size(axis)
    return lax.ppermute(x, axis, [(i, (i + by) % size) for i in range(size)])


def body(residuals, camera_jac, point_jac, obs_index, damping):
    strip_count = lax.axis_size("trk")
    tracks = damping.shape[0]
    rows = residuals.shape[1]
    per_dest = rows // strip_count
    fields = jnp.concatenate(
        [residuals, camera_jac, point_jac, obs_index.astype(jnp.float32)], axis=0
    )
    nf = fields.shape[0]
    send = fields.reshape((nf, strip_count, per_dest)).transpose((1, 0, 2))
    send = send.reshape((strip_count, nf * per_dest))
    send = jnp.roll(send, SHIFT, axis=0)
    got = lax.all_to_all(send, "trk", split_axis=0, concat_axis=0, tiled=True)
    got = got.reshape((strip_count, nf, per_dest)).transpose((1, 0, 2)).reshape((nf, rows))
    position = got[nf - 3].astype(jnp.int32)
    local_slots = rows // tracks
    onehot = (position[:, None] == jnp.arange(rows, dtype=jnp.int32)[None, :]).astype(jnp.float32)
    kept = jnp.concatenate([got[: nf - 3], got[nf - 2 :]], axis=0)
    placed = jnp.dot(kept, onehot, precision=lax.Precision.HIGHEST)
    if CAM_BY_ALL_TO_ALL:
        n_cam = lax.axis_size("cam")
        copies = jnp.broadcast_to(placed[None], (n_cam,) + placed.shape)
        gathered = lax.all_to_all(copies, "cam", 0, 0, tiled=True).transpose((1, 0, 2))
    else:
        gathered = lax.all_gather(placed, "cam", axis=1, tiled=False)
        n_cam = gathered.shape[1]
    damping = from_behind(damping, "trk", SHIFT)
    slots = n_cam * local_slots
    g = gathered.reshape((kept.shape[0], slots, tracks))
    res = g[0:2]
    cj = g[2:20]
    pj = g[20:26]
    cam = g[26].astype(jnp.int32)
    alive = g[27]
    magnitude = jnp.sqrt(res[0] * res[0] + res[1] * res[1])
    w = alive * (HUBER_DELTA / jnp.maximum(magnitude, HUBER_DELTA))
    coup = (cj[:9, None] * pj[None, :3] + cj[9:, None] * pj[None, 3:]) * w
    terms = [
        (w * (pj[k] * pj[l] + pj[3 + k] * pj[3 + l])).sum(axis=0) for k, l in UPPER_PAIRS
    ]
    a, b, c, d, e, f = terms
    a = a + damping
    d = d + damping
    f = f + damping
    cof = [d * f - e * e, c * e - b * f, b * e - c * d, a * f - c * c, b * c - a * e, a * d - b * b]
    det = a * cof[0] + b * cof[1] + c * cof[2]
    sc = [x / det for x in cof]
    inv = [[sc[0], sc[1], sc[2]], [sc[1], sc[3], sc[4]], [sc[2], sc[4], sc[5]]]
    left = jnp.stack(
        [coup[:, 0] * inv[0][l] + coup[:, 1] * inv[1][l] + coup[:, 2] * inv[2][l] for l in range(3)],
        axis=1,
    )
    strip_index = jnp.mod(lax.axis_index("trk") - SHIFT, strip_count)
    column = lax.axis_index("cam")
    visible = jnp.mod(cam // CAMERAS_PER_BLK - 2 * strip_index, 2 * strip_count)
    key = visible * CAMERAS_PER_BLK + cam % CAMERAS_PER_BLK
    owners = HOPS + 1
    grp = jnp.arange(owners * CAMERAS_PER_BLK, dtype=jnp.int32)
    base = (2 * (grp // CAMERAS_PER_BLK)) * CAMERAS_PER_BLK + grp % CAMERAS_PER_BLK
    key_left = base + (column // 2) * CAMERAS_PER_BLK
    key_right = base + (column % 2) * CAMERAS_PER_BLK
    left3 = left.transpose((0, 2, 1, 3)).reshape((9, slots, 3 * tracks))
    coup3 = coup.transpose((0, 2, 1, 3)).reshape((9, slots, 3 * tracks))
    key3 = jnp.tile(key, (1, 3))
    groups = owners * CAMERAS_PER_BLK
    width = owners * TS
    full = (groups, 9, slots, 3 * tracks)

    def panel(keys, values):
        sel = (key3[None] == keys[:, None, None]).astype(jnp.float32)
        sel = jnp.broadcast_to(sel[:, None], full).reshape((width, slots, 3 * tracks))
        vals = jnp.broadcast_to(values[None], full).reshape((width, slots, 3 * tracks))
        return jnp.sum(sel * vals, axis=1)

    left_flat = panel(key_left, left3)
    right_flat = panel(key_right, coup3)
    product = lax.dot_general(
        left_flat, right_flat, (((1,), (1,)), ((), ())), precision=lax.Precision.HIGH
    )
    tiles = product.reshape((owners, TS, owners, TS)).transpose((0, 2, 1, 3))
    tiles = tiles.reshape((owners, owners, TS * TS))
    tile_count = 2 * HOPS + 1
    summed = jnp.zeros((1, 1, tile_count, TS * TS), jnp.float32)
    for distance in range(owners - 1, -1, -1):
        by = distance - SHIFT
        part = tiles[distance][None, None]
        arrived = part if by == 0 else from_behind(part, "trk", by)
        spread = ((0, 0), (0, 0), (HOPS - distance, distance), (0, 0))
        summed = summed + jnp.pad(arrived, spread)
    return summed


def solution(mesh):
    placed = (
        P(None, ("trk", "cam")),
        P(None, ("trk", "cam")),
        P(None, ("trk", "cam")),
        P(None, ("trk", "cam")),
        P("trk"),
    )
    return jax.shard_map(
        body, mesh=mesh, in_specs=placed, out_specs=P("trk", "cam", None, None), check_vma=False
    )
```

```python
import jax
import jax.numpy as jnp
from jax import lax
from jax.sharding import PartitionSpec as P

CAMERAS_PER_BLK = 16
TS = 144
HOPS = 3
SHIFT = 2
CAM_BY_ALL_TO_ALL = True


HUBER_DELTA = 1.0
UPPER_PAIRS = ((0, 0), (0, 1), (0, 2), (1, 1), (1, 2), (2, 2))


def from_behind(x, axis, by):
    size = lax.axis_size(axis)
    return lax.ppermute(x, axis, [(i, (i + by) % size) for i in range(size)])


def body(residuals, camera_jac, point_jac, obs_index, damping):
    strip_count = lax.axis_size("trk")
    tracks = damping.shape[0]
    rows = residuals.shape[1]
    per_dest = rows // strip_count
    fields = jnp.concatenate(
        [residuals, camera_jac, point_jac, obs_index.astype(jnp.float32)], axis=0
    )
    nf = fields.shape[0]
    send = fields.reshape((nf, strip_count, per_dest)).transpose((1, 0, 2))
    send = send.reshape((strip_count, nf * per_dest))
    send = jnp.roll(send, SHIFT, axis=0)
    got = lax.all_to_all(send, "trk", split_axis=0, concat_axis=0, tiled=True)
    got = got.reshape((strip_count, nf, per_dest)).transpose((1, 0, 2)).reshape((nf, rows))
    position = got[nf - 3].astype(jnp.int32)
    local_slots = rows // tracks
    onehot = (position[:, None] == jnp.arange(rows, dtype=jnp.int32)[None, :]).astype(jnp.float32)
    kept = jnp.concatenate([got[: nf - 3], got[nf - 2 :]], axis=0)
    placed = jnp.dot(kept, onehot, precision=lax.Precision.HIGHEST)
    if CAM_BY_ALL_TO_ALL:
        n_cam = lax.axis_size("cam")
        copies = jnp.broadcast_to(placed[None], (n_cam,) + placed.shape)
        gathered = lax.all_to_all(copies, "cam", 0, 0, tiled=True).transpose((1, 0, 2))
    else:
        gathered = lax.all_gather(placed, "cam", axis=1, tiled=False)
        n_cam = gathered.shape[1]
    damping = from_behind(damping, "trk", SHIFT)
    slots = n_cam * local_slots
    g = gathered.reshape((kept.shape[0], slots, tracks))
    res = g[0:2]
    cj = g[2:20]
    pj = g[20:26]
    cam = g[26].astype(jnp.int32)
    alive = g[27]
    magnitude = jnp.sqrt(res[0] * res[0] + res[1] * res[1])
    w = alive * (HUBER_DELTA / jnp.maximum(magnitude, HUBER_DELTA))
    coup = (cj[:9, None] * pj[None, :3] + cj[9:, None] * pj[None, 3:]) * w
    terms = [
        (w * (pj[k] * pj[l] + pj[3 + k] * pj[3 + l])).sum(axis=0) for k, l in UPPER_PAIRS
    ]
    a, b, c, d, e, f = terms
    a = a + damping
    d = d + damping
    f = f + damping
    cof = [d * f - e * e, c * e - b * f, b * e - c * d, a * f - c * c, b * c - a * e, a * d - b * b]
    det = a * cof[0] + b * cof[1] + c * cof[2]
    sc = [x / det for x in cof]
    inv = [[sc[0], sc[1], sc[2]], [sc[1], sc[3], sc[4]], [sc[2], sc[4], sc[5]]]
    left = jnp.stack(
        [coup[:, 0] * inv[0][l] + coup[:, 1] * inv[1][l] + coup[:, 2] * inv[2][l] for l in range(3)],
        axis=1,
    )
    strip_index = jnp.mod(lax.axis_index("trk") - SHIFT, strip_count)
    column = lax.axis_index("cam")
    visible = jnp.mod(cam // CAMERAS_PER_BLK - 2 * strip_index, 2 * strip_count)
    key = visible * CAMERAS_PER_BLK + cam % CAMERAS_PER_BLK
    owners = HOPS + 1
    grp = jnp.arange(owners * CAMERAS_PER_BLK, dtype=jnp.int32)
    base = (2 * (grp // CAMERAS_PER_BLK)) * CAMERAS_PER_BLK + grp % CAMERAS_PER_BLK
    key_left = base + (column // 2) * CAMERAS_PER_BLK
    key_right = base + (column % 2) * CAMERAS_PER_BLK
    left3 = left.transpose((0, 2, 1, 3)).reshape((9, slots, 3 * tracks))
    coup3 = coup.transpose((0, 2, 1, 3)).reshape((9, slots, 3 * tracks))
    key3 = jnp.tile(key, (1, 3))
    groups = owners * CAMERAS_PER_BLK
    width = owners * TS

    def panel(keys, values):
        sel = (key3[None] == keys[:, None, None]).astype(jnp.float32)
        return jnp.sum(sel[None] * values[:, None], axis=2).reshape((width, 3 * tracks))

    new_row = jnp.arange(width, dtype=jnp.int32)
    old_row = (new_row % 9) * groups + new_row // 9
    reorder = (old_row[:, None] == jnp.arange(width, dtype=jnp.int32)[None, :]).astype(jnp.float32)
    left_flat = jnp.dot(reorder, panel(key_left, left3), precision=lax.Precision.HIGH)
    right_flat = jnp.dot(reorder, panel(key_right, coup3), precision=lax.Precision.HIGH)
    left4 = left_flat.reshape((owners, TS, 3 * tracks))
    right4 = right_flat.reshape((owners, TS, 3 * tracks))
    product = lax.dot_general(
        left4, right4, (((2,), (2,)), ((), ())), precision=lax.Precision.HIGH
    )
    tiles = product.transpose((0, 2, 1, 3))
    tiles = tiles.reshape((owners, owners, TS * TS))
    tile_count = 2 * HOPS + 1
    summed = jnp.zeros((tile_count, TS * TS), jnp.float32)
    for distance in range(owners - 1, -1, -1):
        by = distance - SHIFT
        arrived = tiles[distance] if by == 0 else from_behind(tiles[distance], "trk", by)
        summed = summed + jnp.pad(arrived, ((HOPS - distance, distance), (0, 0)))
    return summed.reshape((1, 1, tile_count, TS * TS))


def solution(mesh):
    placed = (
        P(None, ("trk", "cam")),
        P(None, ("trk", "cam")),
        P(None, ("trk", "cam")),
        P(None, ("trk", "cam")),
        P("trk"),
    )
    return jax.shard_map(
        body, mesh=mesh, in_specs=placed, out_specs=P("trk", "cam", None, None), check_vma=False
    )
```

```python
import jax
import jax.numpy as jnp
from jax import lax
from jax.sharding import PartitionSpec as P

CAMERAS_PER_BLK = 16
TS = 144
HOPS = 3
SHIFT = 1
CAM_BY_ALL_TO_ALL = True


HUBER_DELTA = 1.0
UPPER_PAIRS = ((0, 0), (0, 1), (0, 2), (1, 1), (1, 2), (2, 2))


def from_behind(x, axis, by):
    size = lax.axis_size(axis)
    return lax.ppermute(x, axis, [(i, (i + by) % size) for i in range(size)])


def body(residuals, camera_jac, point_jac, obs_index, damping):
    strip_count = lax.axis_size("trk")
    tracks = damping.shape[0]
    rows = residuals.shape[1]
    per_dest = rows // strip_count
    fields = jnp.concatenate(
        [residuals, camera_jac, point_jac, obs_index.astype(jnp.float32)], axis=0
    )
    nf = fields.shape[0]
    send = fields.reshape((nf, strip_count, per_dest)).transpose((1, 0, 2))
    send = send.reshape((strip_count, nf * per_dest))
    send = jnp.roll(send, SHIFT, axis=0)
    got = lax.all_to_all(send, "trk", split_axis=0, concat_axis=0, tiled=True)
    got = got.reshape((strip_count, nf, per_dest)).transpose((1, 0, 2)).reshape((nf, rows))
    position = got[nf - 3].astype(jnp.int32)
    local_slots = rows // tracks
    onehot = (position[:, None] == jnp.arange(rows, dtype=jnp.int32)[None, :]).astype(jnp.float32)
    kept = jnp.concatenate([got[: nf - 3], got[nf - 2 :]], axis=0)
    placed = jnp.dot(kept, onehot, precision=lax.Precision.HIGHEST)
    if CAM_BY_ALL_TO_ALL:
        n_cam = lax.axis_size("cam")
        copies = jnp.broadcast_to(placed[None], (n_cam,) + placed.shape)
        gathered = lax.all_to_all(copies, "cam", 0, 0, tiled=True).transpose((1, 0, 2))
    else:
        gathered = lax.all_gather(placed, "cam", axis=1, tiled=False)
        n_cam = gathered.shape[1]
    damping = from_behind(damping, "trk", SHIFT)
    slots = n_cam * local_slots
    g = gathered.reshape((kept.shape[0], slots, tracks))
    res = g[0:2]
    cj = g[2:20]
    pj = g[20:26]
    cam = g[26].astype(jnp.int32)
    alive = g[27]
    magnitude = jnp.sqrt(res[0] * res[0] + res[1] * res[1])
    w = alive * (HUBER_DELTA / jnp.maximum(magnitude, HUBER_DELTA))
    coup = (cj[:9, None] * pj[None, :3] + cj[9:, None] * pj[None, 3:]) * w
    terms = [
        (w * (pj[k] * pj[l] + pj[3 + k] * pj[3 + l])).sum(axis=0) for k, l in UPPER_PAIRS
    ]
    a, b, c, d, e, f = terms
    a = a + damping
    d = d + damping
    f = f + damping
    cof = [d * f - e * e, c * e - b * f, b * e - c * d, a * f - c * c, b * c - a * e, a * d - b * b]
    det = a * cof[0] + b * cof[1] + c * cof[2]
    sc = [x / det for x in cof]
    inv = [[sc[0], sc[1], sc[2]], [sc[1], sc[3], sc[4]], [sc[2], sc[4], sc[5]]]
    left = jnp.stack(
        [coup[:, 0] * inv[0][l] + coup[:, 1] * inv[1][l] + coup[:, 2] * inv[2][l] for l in range(3)],
        axis=1,
    )
    strip_index = jnp.mod(lax.axis_index("trk") - SHIFT, strip_count)
    column = lax.axis_index("cam")
    visible = jnp.mod(cam // CAMERAS_PER_BLK - 2 * strip_index, 2 * strip_count)
    key = visible * CAMERAS_PER_BLK + cam % CAMERAS_PER_BLK
    owners = HOPS + 1
    grp = jnp.arange(owners * CAMERAS_PER_BLK, dtype=jnp.int32)
    base = (2 * (grp // CAMERAS_PER_BLK)) * CAMERAS_PER_BLK + grp % CAMERAS_PER_BLK
    key_left = base + (column // 2) * CAMERAS_PER_BLK
    key_right = base + (column % 2) * CAMERAS_PER_BLK
    left3 = left.transpose((0, 2, 1, 3)).reshape((9, slots, 3 * tracks))
    coup3 = coup.transpose((0, 2, 1, 3)).reshape((9, slots, 3 * tracks))
    key3 = jnp.tile(key, (1, 3))
    groups = owners * CAMERAS_PER_BLK
    width = owners * TS
    full = (groups, 9, slots, 3 * tracks)

    def panel(keys, values):
        sel = (key3[None] == keys[:, None, None]).astype(jnp.float32)
        sel = jnp.broadcast_to(sel[:, None], full).reshape((width, slots, 3 * tracks))
        vals = jnp.broadcast_to(values[None], full).reshape((width, slots, 3 * tracks))
        return jnp.sum(sel * vals, axis=1)

    left_flat = panel(key_left, left3)
    right_flat = panel(key_right, coup3)
    product = lax.dot_general(
        left_flat, right_flat, (((1,), (1,)), ((), ())), precision=lax.Precision.HIGH
    )
    tiles = product.reshape((owners, TS, owners, TS)).transpose((0, 2, 1, 3))
    tiles = tiles.reshape((owners, owners, TS * TS))
    tile_count = 2 * HOPS + 1
    summed = jnp.zeros((tile_count, TS * TS), jnp.float32)
    for distance in range(owners - 1, -1, -1):
        by = distance - SHIFT
        arrived = tiles[distance] if by == 0 else from_behind(tiles[distance], "trk", by)
        summed = summed + jnp.pad(arrived, ((HOPS - distance, distance), (0, 0)))
    return summed.reshape((1, 1, tile_count, TS * TS))


def solution(mesh):
    placed = (
        P(None, ("trk", "cam")),
        P(None, ("trk", "cam")),
        P(None, ("trk", "cam")),
        P(None, ("trk", "cam")),
        P("trk"),
    )
    return jax.shard_map(
        body, mesh=mesh, in_specs=placed, out_specs=P("trk", "cam", None, None), check_vma=False
    )
```

```python
import jax
import jax.numpy as jnp
from jax import lax
from jax.sharding import PartitionSpec as P

CAMERAS_PER_BLK = 16
TS = 144
HOPS = 3
SHIFT = 2
CAM_BY_ALL_TO_ALL = True


HUBER_DELTA = 1.0
UPPER_PAIRS = ((0, 0), (0, 1), (0, 2), (1, 1), (1, 2), (2, 2))


def from_behind(x, axis, by):
    size = lax.axis_size(axis)
    return lax.ppermute(x, axis, [(i, (i + by) % size) for i in range(size)])


def body(residuals, camera_jac, point_jac, obs_index, damping):
    strip_count = lax.axis_size("trk")
    tracks = damping.shape[0]
    rows = residuals.shape[1]
    per_dest = rows // strip_count
    fields = jnp.concatenate(
        [residuals, camera_jac, point_jac, obs_index.astype(jnp.float32)], axis=0
    )
    nf = fields.shape[0]
    send = fields.reshape((nf, strip_count, per_dest)).transpose((1, 0, 2))
    send = send.reshape((strip_count, nf * per_dest))
    send = jnp.roll(send, SHIFT, axis=0)
    got = lax.all_to_all(send, "trk", split_axis=0, concat_axis=0, tiled=True)
    got = got.reshape((strip_count, nf, per_dest)).transpose((1, 0, 2)).reshape((nf, rows))
    position = got[nf - 3].astype(jnp.int32)
    local_slots = rows // tracks
    onehot = (position[:, None] == jnp.arange(rows, dtype=jnp.int32)[None, :]).astype(jnp.float32)
    magnitude = jnp.sqrt(got[0] * got[0] + got[1] * got[1])
    weight = got[nf - 1] * (HUBER_DELTA / jnp.maximum(magnitude, HUBER_DELTA))
    kept = jnp.concatenate([got[2 : nf - 3], weight[None], got[nf - 2 : nf - 1]], axis=0)
    placed = jnp.dot(kept, onehot, precision=lax.Precision.HIGHEST)
    if CAM_BY_ALL_TO_ALL:
        n_cam = lax.axis_size("cam")
        copies = jnp.broadcast_to(placed[None], (n_cam,) + placed.shape)
        gathered = lax.all_to_all(copies, "cam", 0, 0, tiled=True).transpose((1, 0, 2))
    else:
        gathered = lax.all_gather(placed, "cam", axis=1, tiled=False)
        n_cam = gathered.shape[1]
    damping = from_behind(damping, "trk", SHIFT)
    slots = n_cam * local_slots
    g = gathered.reshape((kept.shape[0], slots, tracks))
    cj = g[0:18]
    pj = g[18:24]
    w = g[24]
    cam = g[25].astype(jnp.int32)
    coup = (cj[:9, None] * pj[None, :3] + cj[9:, None] * pj[None, 3:]) * w
    terms = [
        (w * (pj[k] * pj[l] + pj[3 + k] * pj[3 + l])).sum(axis=0) for k, l in UPPER_PAIRS
    ]
    a, b, c, d, e, f = terms
    a = a + damping
    d = d + damping
    f = f + damping
    cof = [d * f - e * e, c * e - b * f, b * e - c * d, a * f - c * c, b * c - a * e, a * d - b * b]
    det = a * cof[0] + b * cof[1] + c * cof[2]
    sc = [x / det for x in cof]
    inv = [[sc[0], sc[1], sc[2]], [sc[1], sc[3], sc[4]], [sc[2], sc[4], sc[5]]]
    left = jnp.stack(
        [coup[:, 0] * inv[0][l] + coup[:, 1] * inv[1][l] + coup[:, 2] * inv[2][l] for l in range(3)],
        axis=1,
    )
    strip_index = jnp.mod(lax.axis_index("trk") - SHIFT, strip_count)
    column = lax.axis_index("cam")
    visible = jnp.mod(cam // CAMERAS_PER_BLK - 2 * strip_index, 2 * strip_count)
    key = visible * CAMERAS_PER_BLK + cam % CAMERAS_PER_BLK
    owners = HOPS + 1
    grp = jnp.arange(owners * CAMERAS_PER_BLK, dtype=jnp.int32)
    base = (2 * (grp // CAMERAS_PER_BLK)) * CAMERAS_PER_BLK + grp % CAMERAS_PER_BLK
    key_left = base + (column // 2) * CAMERAS_PER_BLK
    key_right = base + (column % 2) * CAMERAS_PER_BLK
    left3 = left.transpose((0, 2, 1, 3)).reshape((9, slots, 3 * tracks))
    coup3 = coup.transpose((0, 2, 1, 3)).reshape((9, slots, 3 * tracks))
    key3 = jnp.tile(key, (1, 3))
    groups = owners * CAMERAS_PER_BLK
    width = owners * TS
    full = (groups, 9, slots, 3 * tracks)

    def panel(keys, values):
        sel = (key3[None] == keys[:, None, None]).astype(jnp.float32)
        sel = jnp.broadcast_to(sel[:, None], full).reshape((width, slots, 3 * tracks))
        vals = jnp.broadcast_to(values[None], full).reshape((width, slots, 3 * tracks))
        return jnp.sum(sel * vals, axis=1)

    left_flat = panel(key_left, left3)
    right_flat = panel(key_right, coup3)
    product = lax.dot_general(
        left_flat, right_flat, (((1,), (1,)), ((), ())), precision=lax.Precision.HIGH
    )
    tiles = product.reshape((owners, TS, owners, TS)).transpose((0, 2, 1, 3))
    tiles = tiles.reshape((owners, owners, TS * TS))
    tile_count = 2 * HOPS + 1
    summed = jnp.zeros((tile_count, TS * TS), jnp.float32)
    for distance in range(owners - 1, -1, -1):
        by = distance - SHIFT
        arrived = tiles[distance] if by == 0 else from_behind(tiles[distance], "trk", by)
        summed = summed + jnp.pad(arrived, ((HOPS - distance, distance), (0, 0)))
    return summed.reshape((1, 1, tile_count, TS * TS))


def solution(mesh):
    placed = (
        P(None, ("trk", "cam")),
        P(None, ("trk", "cam")),
        P(None, ("trk", "cam")),
        P(None, ("trk", "cam")),
        P("trk"),
    )
    return jax.shard_map(
        body, mesh=mesh, in_specs=placed, out_specs=P("trk", "cam", None, None), check_vma=False
    )
```

```python
import jax
import jax.numpy as jnp
from jax import lax
from jax.sharding import PartitionSpec as P

CAMERAS_PER_BLK = 16
TS = 144
HOPS = 3
SHIFT = 2
CAM_BY_ALL_TO_ALL = True


HUBER_DELTA = 1.0
UPPER_PAIRS = ((0, 0), (0, 1), (0, 2), (1, 1), (1, 2), (2, 2))


def from_behind(x, axis, by):
    size = lax.axis_size(axis)
    return lax.ppermute(x, axis, [(i, (i + by) % size) for i in range(size)])


def body(residuals, camera_jac, point_jac, obs_index, damping):
    strip_count = lax.axis_size("trk")
    tracks = damping.shape[0]
    rows = residuals.shape[1]
    per_dest = rows // strip_count
    fields = jnp.concatenate(
        [residuals, camera_jac, point_jac, obs_index.astype(jnp.float32)], axis=0
    )
    nf = fields.shape[0]
    send = fields.reshape((nf, strip_count, per_dest)).transpose((1, 0, 2))
    send = send.reshape((strip_count, nf * per_dest))
    send = jnp.roll(send, SHIFT, axis=0)
    got = lax.all_to_all(send, "trk", split_axis=0, concat_axis=0, tiled=True)
    got = got.reshape((strip_count, nf, per_dest)).transpose((1, 0, 2)).reshape((nf, rows))
    position = got[nf - 3].astype(jnp.int32)
    local_slots = rows // tracks
    onehot = (position[:, None] == jnp.arange(rows, dtype=jnp.int32)[None, :]).astype(jnp.float32)
    kept = jnp.concatenate([got[: nf - 3], got[nf - 2 :]], axis=0)
    placed = jnp.dot(kept, onehot, precision=lax.Precision.HIGH)
    if CAM_BY_ALL_TO_ALL:
        n_cam = lax.axis_size("cam")
        copies = jnp.broadcast_to(placed[None], (n_cam,) + placed.shape)
        gathered = lax.all_to_all(copies, "cam", 0, 0, tiled=True).transpose((1, 0, 2))
    else:
        gathered = lax.all_gather(placed, "cam", axis=1, tiled=False)
        n_cam = gathered.shape[1]
    damping = from_behind(damping, "trk", SHIFT)
    slots = n_cam * local_slots
    g = gathered.reshape((kept.shape[0], slots, tracks))
    res = g[0:2]
    cj = g[2:20]
    pj = g[20:26]
    cam = g[26].astype(jnp.int32)
    alive = g[27]
    magnitude = jnp.sqrt(res[0] * res[0] + res[1] * res[1])
    w = alive * (HUBER_DELTA / jnp.maximum(magnitude, HUBER_DELTA))
    coup = (cj[:9, None] * pj[None, :3] + cj[9:, None] * pj[None, 3:]) * w
    terms = [
        (w * (pj[k] * pj[l] + pj[3 + k] * pj[3 + l])).sum(axis=0) for k, l in UPPER_PAIRS
    ]
    a, b, c, d, e, f = terms
    a = a + damping
    d = d + damping
    f = f + damping
    cof = [d * f - e * e, c * e - b * f, b * e - c * d, a * f - c * c, b * c - a * e, a * d - b * b]
    det = a * cof[0] + b * cof[1] + c * cof[2]
    sc = [x / det for x in cof]
    inv = [[sc[0], sc[1], sc[2]], [sc[1], sc[3], sc[4]], [sc[2], sc[4], sc[5]]]
    left = jnp.stack(
        [coup[:, 0] * inv[0][l] + coup[:, 1] * inv[1][l] + coup[:, 2] * inv[2][l] for l in range(3)],
        axis=1,
    )
    strip_index = jnp.mod(lax.axis_index("trk") - SHIFT, strip_count)
    column = lax.axis_index("cam")
    visible = jnp.mod(cam // CAMERAS_PER_BLK - 2 * strip_index, 2 * strip_count)
    key = visible * CAMERAS_PER_BLK + cam % CAMERAS_PER_BLK
    owners = HOPS + 1
    grp = jnp.arange(owners * CAMERAS_PER_BLK, dtype=jnp.int32)
    base = (2 * (grp // CAMERAS_PER_BLK)) * CAMERAS_PER_BLK + grp % CAMERAS_PER_BLK
    key_left = base + (column // 2) * CAMERAS_PER_BLK
    key_right = base + (column % 2) * CAMERAS_PER_BLK
    left3 = left.transpose((0, 2, 1, 3)).reshape((9, slots, 3 * tracks))
    coup3 = coup.transpose((0, 2, 1, 3)).reshape((9, slots, 3 * tracks))
    key3 = jnp.tile(key, (1, 3))
    groups = owners * CAMERAS_PER_BLK
    width = owners * TS
    full = (groups, 9, slots, 3 * tracks)

    def panel(keys, values):
        sel = (key3[None] == keys[:, None, None]).astype(jnp.float32)
        sel = jnp.broadcast_to(sel[:, None], full).reshape((width, slots, 3 * tracks))
        vals = jnp.broadcast_to(values[None], full).reshape((width, slots, 3 * tracks))
        return jnp.sum(sel * vals, axis=1)

    left_flat = panel(key_left, left3)
    right_flat = panel(key_right, coup3)
    product = lax.dot_general(
        left_flat, right_flat, (((1,), (1,)), ((), ())), precision=lax.Precision.HIGH
    )
    tiles = product.reshape((owners, TS, owners, TS)).transpose((0, 2, 1, 3))
    tiles = tiles.reshape((owners, owners, TS * TS))
    tile_count = 2 * HOPS + 1
    summed = jnp.zeros((tile_count, TS * TS), jnp.float32)
    for distance in range(owners - 1, -1, -1):
        by = distance - SHIFT
        arrived = tiles[distance] if by == 0 else from_behind(tiles[distance], "trk", by)
        summed = summed + jnp.pad(arrived, ((HOPS - distance, distance), (0, 0)))
    return summed.reshape((1, 1, tile_count, TS * TS))


def solution(mesh):
    placed = (
        P(None, ("trk", "cam")),
        P(None, ("trk", "cam")),
        P(None, ("trk", "cam")),
        P(None, ("trk", "cam")),
        P("trk"),
    )
    return jax.shard_map(
        body, mesh=mesh, in_specs=placed, out_specs=P("trk", "cam", None, None), check_vma=False
    )
```

```python
import jax
import jax.numpy as jnp
from jax import lax
from jax.sharding import PartitionSpec as P

CAMERAS_PER_BLK = 16
TS = 144
HOPS = 3
SHIFT = 2
CAM_BY_ALL_TO_ALL = True


HUBER_DELTA = 1.0
UPPER_PAIRS = ((0, 0), (0, 1), (0, 2), (1, 1), (1, 2), (2, 2))


def from_behind(x, axis, by):
    size = lax.axis_size(axis)
    return lax.ppermute(x, axis, [(i, (i + by) % size) for i in range(size)])


def body(residuals, camera_jac, point_jac, obs_index, damping):
    strip_count = lax.axis_size("trk")
    tracks = damping.shape[0]
    rows = residuals.shape[1]
    per_dest = rows // strip_count
    fields = jnp.concatenate(
        [residuals, camera_jac, point_jac, obs_index.astype(jnp.float32)], axis=0
    )
    nf = fields.shape[0]
    send = fields.reshape((nf, strip_count, per_dest)).transpose((1, 0, 2))
    send = send.reshape((strip_count, nf * per_dest))
    send = jnp.roll(send, SHIFT, axis=0)
    got = lax.all_to_all(send, "trk", split_axis=0, concat_axis=0, tiled=True)
    got = got.reshape((strip_count, nf, per_dest)).transpose((1, 0, 2)).reshape((nf, rows))
    position = got[nf - 3].astype(jnp.int32)
    local_slots = rows // tracks
    onehot = (position[:, None] == jnp.arange(rows, dtype=jnp.int32)[None, :]).astype(jnp.float32)
    magnitude = jnp.sqrt(got[0] * got[0] + got[1] * got[1])
    weight = got[nf - 1] * (HUBER_DELTA / jnp.maximum(magnitude, HUBER_DELTA))
    kept = jnp.concatenate([got[2 : nf - 3], weight[None], got[nf - 2 : nf - 1]], axis=0)
    placed = jnp.dot(kept, onehot, precision=lax.Precision.HIGH)
    if CAM_BY_ALL_TO_ALL:
        n_cam = lax.axis_size("cam")
        copies = jnp.broadcast_to(placed[None], (n_cam,) + placed.shape)
        gathered = lax.all_to_all(copies, "cam", 0, 0, tiled=True).transpose((1, 0, 2))
    else:
        gathered = lax.all_gather(placed, "cam", axis=1, tiled=False)
        n_cam = gathered.shape[1]
    damping = from_behind(damping, "trk", SHIFT)
    slots = n_cam * local_slots
    g = gathered.reshape((kept.shape[0], slots, tracks))
    cj = g[0:18]
    pj = g[18:24]
    w = g[24]
    cam = g[25].astype(jnp.int32)
    coup = (cj[:9, None] * pj[None, :3] + cj[9:, None] * pj[None, 3:]) * w
    terms = [
        (w * (pj[k] * pj[l] + pj[3 + k] * pj[3 + l])).sum(axis=0) for k, l in UPPER_PAIRS
    ]
    a, b, c, d, e, f = terms
    a = a + damping
    d = d + damping
    f = f + damping
    cof = [d * f - e * e, c * e - b * f, b * e - c * d, a * f - c * c, b * c - a * e, a * d - b * b]
    det = a * cof[0] + b * cof[1] + c * cof[2]
    sc = [x / det for x in cof]
    inv = [[sc[0], sc[1], sc[2]], [sc[1], sc[3], sc[4]], [sc[2], sc[4], sc[5]]]
    left = jnp.stack(
        [coup[:, 0] * inv[0][l] + coup[:, 1] * inv[1][l] + coup[:, 2] * inv[2][l] for l in range(3)],
        axis=1,
    )
    strip_index = jnp.mod(lax.axis_index("trk") - SHIFT, strip_count)
    column = lax.axis_index("cam")
    visible = jnp.mod(cam // CAMERAS_PER_BLK - 2 * strip_index, 2 * strip_count)
    key = visible * CAMERAS_PER_BLK + cam % CAMERAS_PER_BLK
    owners = HOPS + 1
    grp = jnp.arange(owners * CAMERAS_PER_BLK, dtype=jnp.int32)
    base = (2 * (grp // CAMERAS_PER_BLK)) * CAMERAS_PER_BLK + grp % CAMERAS_PER_BLK
    key_left = base + (column // 2) * CAMERAS_PER_BLK
    key_right = base + (column % 2) * CAMERAS_PER_BLK
    left3 = left.transpose((0, 2, 1, 3)).reshape((9, slots, 3 * tracks))
    coup3 = coup.transpose((0, 2, 1, 3)).reshape((9, slots, 3 * tracks))
    key3 = jnp.tile(key, (1, 3))
    groups = owners * CAMERAS_PER_BLK
    width = owners * TS
    full = (groups, 9, slots, 3 * tracks)

    def panel(keys, values):
        sel = (key3[None] == keys[:, None, None]).astype(jnp.float32)
        sel = jnp.broadcast_to(sel[:, None], full).reshape((width, slots, 3 * tracks))
        vals = jnp.broadcast_to(values[None], full).reshape((width, slots, 3 * tracks))
        return jnp.sum(sel * vals, axis=1)

    left_flat = panel(key_left, left3)
    right_flat = panel(key_right, coup3)
    product = lax.dot_general(
        left_flat, right_flat, (((1,), (1,)), ((), ())), precision=lax.Precision.HIGH
    )
    tiles = product.reshape((owners, TS, owners, TS)).transpose((0, 2, 1, 3))
    tiles = tiles.reshape((owners, owners, TS * TS))
    tile_count = 2 * HOPS + 1
    summed = jnp.zeros((tile_count, TS * TS), jnp.float32)
    for distance in range(owners - 1, -1, -1):
        by = distance - SHIFT
        arrived = tiles[distance] if by == 0 else from_behind(tiles[distance], "trk", by)
        summed = summed + jnp.pad(arrived, ((HOPS - distance, distance), (0, 0)))
    return summed.reshape((1, 1, tile_count, TS * TS))


def solution(mesh):
    placed = (
        P(None, ("trk", "cam")),
        P(None, ("trk", "cam")),
        P(None, ("trk", "cam")),
        P(None, ("trk", "cam")),
        P("trk"),
    )
    return jax.shard_map(
        body, mesh=mesh, in_specs=placed, out_specs=P("trk", "cam", None, None), check_vma=False
    )
```

```python
import jax
import jax.numpy as jnp
from jax import lax
from jax.sharding import PartitionSpec as P

CAMERAS_PER_BLK = 16
TS = 144
HOPS = 3
SHIFT = 2
CAM_BY_ALL_TO_ALL = True


HUBER_DELTA = 1.0
UPPER_PAIRS = ((0, 0), (0, 1), (0, 2), (1, 1), (1, 2), (2, 2))


def from_behind(x, axis, by):
    size = lax.axis_size(axis)
    return lax.ppermute(x, axis, [(i, (i + by) % size) for i in range(size)])


def body(residuals, camera_jac, point_jac, obs_index, damping):
    strip_count = lax.axis_size("trk")
    tracks = damping.shape[0]
    rows = residuals.shape[1]
    per_dest = rows // strip_count
    fields = jnp.concatenate(
        [residuals, camera_jac, point_jac, obs_index.astype(jnp.float32)], axis=0
    )
    nf = fields.shape[0]
    send = fields.reshape((nf, strip_count, per_dest)).transpose((1, 0, 2))
    send = send.reshape((strip_count, nf * per_dest))
    send = jnp.roll(send, SHIFT, axis=0)
    got = lax.all_to_all(send, "trk", split_axis=0, concat_axis=0, tiled=True)
    got = got.reshape((strip_count, nf, per_dest)).transpose((1, 0, 2)).reshape((nf, rows))
    position = got[nf - 3].astype(jnp.int32)
    local_slots = rows // tracks
    onehot = (position[:, None] == jnp.arange(rows, dtype=jnp.int32)[None, :]).astype(jnp.float32)
    kept = jnp.concatenate([got[: nf - 3], got[nf - 2 :]], axis=0)
    placed = jnp.dot(kept, onehot, precision=lax.Precision.HIGH)
    if CAM_BY_ALL_TO_ALL:
        n_cam = lax.axis_size("cam")
        copies = jnp.broadcast_to(placed[None], (n_cam,) + placed.shape)
        gathered = lax.all_to_all(copies, "cam", 0, 0, tiled=True).transpose((1, 0, 2))
    else:
        gathered = lax.all_gather(placed, "cam", axis=1, tiled=False)
        n_cam = gathered.shape[1]
    damping = from_behind(damping, "trk", SHIFT)
    slots = n_cam * local_slots
    g = gathered.reshape((kept.shape[0], slots, tracks))
    res = g[0:2]
    cj = g[2:20]
    pj = g[20:26]
    cam = g[26].astype(jnp.int32)
    alive = g[27]
    magnitude = jnp.sqrt(res[0] * res[0] + res[1] * res[1])
    w = alive * (HUBER_DELTA / jnp.maximum(magnitude, HUBER_DELTA))
    coup = (cj[:9, None] * pj[None, :3] + cj[9:, None] * pj[None, 3:]) * w
    terms = [
        (w * (pj[k] * pj[l] + pj[3 + k] * pj[3 + l])).sum(axis=0) for k, l in UPPER_PAIRS
    ]
    a, b, c, d, e, f = terms
    a = a + damping
    d = d + damping
    f = f + damping
    cof = [d * f - e * e, c * e - b * f, b * e - c * d, a * f - c * c, b * c - a * e, a * d - b * b]
    det = a * cof[0] + b * cof[1] + c * cof[2]
    sc = [x / det for x in cof]
    inv = [[sc[0], sc[1], sc[2]], [sc[1], sc[3], sc[4]], [sc[2], sc[4], sc[5]]]
    left = jnp.stack(
        [coup[:, 0] * inv[0][l] + coup[:, 1] * inv[1][l] + coup[:, 2] * inv[2][l] for l in range(3)],
        axis=1,
    )
    strip_index = jnp.mod(lax.axis_index("trk") - SHIFT, strip_count)
    column = lax.axis_index("cam")
    visible = jnp.mod(cam // CAMERAS_PER_BLK - 2 * strip_index, 2 * strip_count)
    key = visible * CAMERAS_PER_BLK + cam % CAMERAS_PER_BLK
    owners = HOPS + 1
    grp = jnp.arange(owners * CAMERAS_PER_BLK, dtype=jnp.int32)
    base = (2 * (grp // CAMERAS_PER_BLK)) * CAMERAS_PER_BLK + grp % CAMERAS_PER_BLK
    key_left = base + (column // 2) * CAMERAS_PER_BLK
    key_right = base + (column % 2) * CAMERAS_PER_BLK
    left3 = left.transpose((0, 2, 1, 3)).reshape((9, slots, 3 * tracks))
    coup3 = coup.transpose((0, 2, 1, 3)).reshape((9, slots, 3 * tracks))
    key3 = jnp.tile(key, (1, 3))
    groups = owners * CAMERAS_PER_BLK
    width = owners * TS
    full = (groups, 9, slots, 3 * tracks)

    def panel(keys, values):
        sel = (key3[None] == keys[:, None, None]).astype(jnp.float32)
        sel = jnp.broadcast_to(sel[:, None], full).reshape((width, slots, 3 * tracks))
        vals = jnp.broadcast_to(values[None], full).reshape((width, slots, 3 * tracks))
        return jnp.sum(sel * vals, axis=1)

    left_flat = panel(key_left, left3)
    right_flat = panel(key_right, coup3)
    product = lax.dot_general(
        left_flat, right_flat, (((1,), (1,)), ((), ())), precision=lax.Precision.HIGH
    )
    tiles = product.reshape((owners, TS, owners, TS)).transpose((0, 2, 1, 3))
    tiles = tiles.reshape((owners, owners, TS * TS))
    tile_count = 2 * HOPS + 1
    summed = jnp.zeros((1, 1, tile_count, TS * TS), jnp.float32)
    for distance in range(owners - 1, -1, -1):
        by = distance - SHIFT
        part = tiles[distance][None, None]
        arrived = part if by == 0 else from_behind(part, "trk", by)
        spread = ((0, 0), (0, 0), (HOPS - distance, distance), (0, 0))
        summed = summed + jnp.pad(arrived, spread)
    return summed


def solution(mesh):
    placed = (
        P(None, ("trk", "cam")),
        P(None, ("trk", "cam")),
        P(None, ("trk", "cam")),
        P(None, ("trk", "cam")),
        P("trk"),
    )
    return jax.shard_map(
        body, mesh=mesh, in_specs=placed, out_specs=P("trk", "cam", None, None), check_vma=False
    )
```
